512 devices in a mesh: seq: 64 (over x, z_lo, y), tp: 8 (over z_hi, core).
Axes of the slice: x: 4, y: 8, z: 8 (z_hi: 4, z_lo: 2; z = z_hi * 2 + z_lo), core: 2. Of those that a mesh axis runs over, the one named last changes fastest.
Arguments:
- tokens: bfloat16 [16384, 2048], P('seq', 'tp'), may hold values from -6 to 6
- key_weight: bfloat16 [2048, 2048], P(None, 'tp'), may hold values from -0.125 to 0.125
- value_weight: bfloat16 [2048, 2048], P(None, 'tp'), may hold values from -0.125 to 0.125
- queries: bfloat16 [16384, 2, 2048], P('seq', None, 'tp'), may hold values from -256 to 256
- prompt_pages: int32 [16], replicated, may hold values from 1 to 97, 1024 in all
- page_table: int32 [1024], P('seq'), may hold values from 0 to 1023, as said below
Outputs:
- attended: bfloat16 [16384, 2, 2048], P('seq', None, 'tp')
- cache: bfloat16 [1024, 16, 2, 2048], P('seq', None, None, 'tp')
The draws below stay inside these ranges and needn't reach their ends.
Inputs may be any that keep to these rules, and one draw needn't show every extreme that they name: `prompt_pages`: lengths of the prompts in pages; they sum to 1024 and the longest has exactly 97 pages. `page_table`: A permutation of the cache pages. Page c is held by owner c // 16 of seq. At most 1 pages of one stream block go to one owner, some block sends exactly 1 to one owner, and every owner receives 256/16 pages.
All inputs are finite; a program needn't handle non-finite values.
Results may differ from the reference program's by a relative error of at most 0.03.
Values may be sent and summed in bfloat16 or wider, within the bound.
No kernel may reach another device: no remote copies, remote signals or barrier semaphores. Data moves between devices by JAX's collectives and lax.ppermute only.
A program may use at most 64 MiB of HBM per device.

```python
import math
import jax
import jax.numpy as jnp
import numpy as np
from jax import lax

D = 2048
KV_HEADS = 16
HD = 128
TOPK = 2
PAGE = 16
BACK = 6
TOK_DEV = 256
TOKENS = 16384
KVW = 2048
MOST = 1552
PROMPTS = 16
POOL = 1024


def draw_queries(key, part):
    shape = (TOKENS, TOPK, KVW)
    return jnp.clip(jax.random.normal(key, shape, jnp.float32), -6.0, 6.0).astype(jnp.bfloat16)


def draw_page_table(key, part):
    pages_dev = TOK_DEV // PAGE
    owners = POOL // pages_dev
    first_key, second_key, third_key = jax.random.split(jax.random.fold_in(key, 11), 3)
    mixed = jax.random.permutation(first_key, owners)
    rank_key = jnp.where(mixed == 1, 0, jnp.where(mixed == owners // 2, 1, 2)).astype(jnp.int32)
    order = jnp.argsort(rank_key, stable=True)
    front = mixed[order]
    used = min(pages_dev, owners)
    roll_by = jax.random.randint(third_key, (), 0, max(1, used - 1))
    shifts = jnp.roll(front, roll_by)
    stream_page = jnp.arange(POOL)
    source = stream_page // pages_dev
    within = stream_page % pages_dev
    owner = (source + shifts[within % owners]) % owners
    owner_keys = jax.random.split(second_key, owners)
    orders = jax.vmap(lambda one_key: jax.random.permutation(one_key, pages_dev))(owner_keys)
    place_on_owner = orders[owner, within]
    return (owner * pages_dev + place_on_owner).astype(jnp.int32)


def level_of(stream_key, extent, pieces, least, largest):
    def one(axis_at, blocks):
        draws = jax.random.uniform(jax.random.fold_in(jax.random.fold_in(stream_key, 6), axis_at), (blocks,), jnp.float32, least / len(pieces), largest / len(pieces))
        return jnp.repeat(jnp.exp(draws), extent[axis_at] // blocks).reshape((-1,) + (1,) * (len(extent) - axis_at - 1))

    factor_of = one(*pieces[0])
    for cut in pieces[1:]:
        factor_of = factor_of * one(*cut)
    return factor_of


def split_up(amount, total, most, slope):
    portions = [(1 << 20) // math.isqrt(grade ** slope) + 1 for grade in range(2, amount + 1)]
    spare, given = total - most - (amount - 1), [1] * (amount - 1)
    while spare > 0:
        movable = [i for i in range(amount - 1) if given[i] < most]
        pool, left = sum([portions[i] for i in movable]), spare
        for i in movable:
            more = min(most - given[i], max(1, left * portions[i] // pool), spare)
            given[i] = given[i] + more
            spare = spare - more
    return np.array([most] + given)


def ragged(stream_key, count, total, most, slope):
    if count == 2:
        one = jax.random.randint(stream_key, (), max(1, total - most), min(most, total - 1) + 1)
        return jnp.stack([one, total - one])
    tallies = jnp.asarray(split_up(count, total, most, slope), jnp.int32)
    pairs = (count - 1) // 2
    giver, receiver = tallies[1:1 + 2 * pairs:2], tallies[2:2 + 2 * pairs:2]
    room = jnp.minimum(giver - 1, most - receiver)
    moved = jax.random.randint(jax.random.fold_in(stream_key, 1), (pairs,), 0, 1 << 20) % (room + 1)
    tallies = tallies.at[1:1 + 2 * pairs:2].set(giver - moved).at[2:2 + 2 * pairs:2].set(receiver + moved)
    return tallies[jax.random.permutation(jax.random.fold_in(stream_key, 2), count)]


def noise(key, extent, scale, limit, cuts=(), held_as=jnp.bfloat16):
    factor_of = level_of(key, extent, cuts, -0.22, 0.18) if cuts else 1.0
    result = jax.random.normal(key, extent, jnp.float32) * scale * factor_of
    return jnp.minimum(jnp.maximum(result, -limit), limit).astype(held_as)


def setup_inputs(seed: int = 0) -> dict:
    key_list = jax.random.split(jax.random.key(seed), 7)
    tokens = noise(key_list[0], (TOKENS, D), 1.0, 6.0, ((0, 64), (1, 8)))
    key_weight = noise(key_list[1], (D, KVW), D ** -0.5, 0.125, ((1, 8),))
    value_weight = noise(key_list[2], (D, KVW), D ** -0.5, 0.125, ((1, 8),))
    queries = draw_queries(jax.random.fold_in(key_list[6], 71), 0)
    prompt_pages = ragged(key_list[4], PROMPTS, POOL, MOST // PAGE, 2).astype(jnp.int32)
    page_table = draw_page_table(jax.random.fold_in(key_list[6], 71), 0)
    return dict(tokens=tokens, key_weight=key_weight, value_weight=value_weight, queries=queries, prompt_pages=prompt_pages, page_table=page_table)


def segment_info(positions, prompt_pages):
    ends = (PAGE * jnp.cumsum(prompt_pages)).astype(jnp.int32)
    below = ends[None, :] <= positions[:, None]
    segment = lax.optimization_barrier(jnp.sum(below.astype(jnp.int32), axis=1)).astype(jnp.int32)
    start = lax.optimization_barrier(jnp.max(jnp.where(below, ends[None, :], 0), axis=1)).astype(jnp.int32)
    return (segment, (positions - start).astype(jnp.int32))

def rotate_heads(raw, offsets):
    half = HD // 2
    inverse = 10000.0 ** (-(2.0 * jnp.arange(half, dtype=jnp.float32)) / HD)
    angle = offsets.astype(jnp.float32)[:, None] * inverse[None, :]
    cosine = jnp.cos(angle)[:, None, :]
    sine = jnp.sin(angle)[:, None, :]
    lower = raw[..., :half]
    upper = raw[..., half:]
    return jnp.concatenate([lower * cosine - upper * sine, upper * cosine + lower * sine], axis=-1)

def reference(tokens, key_weight, value_weight, queries, prompt_pages, page_table):
    positions = jnp.arange(TOKENS, dtype=jnp.int32)
    segment, offsets = segment_info(positions, prompt_pages)
    raw_keys = jnp.dot(tokens, key_weight, preferred_element_type=jnp.float32).reshape(TOKENS, KV_HEADS, HD)
    keys = rotate_heads(raw_keys, offsets).astype(jnp.bfloat16)
    values = jnp.dot(tokens, value_weight, preferred_element_type=jnp.float32).astype(jnp.bfloat16)
    values = values.reshape(TOKENS, KV_HEADS, HD)
    reach = BACK * TOK_DEV
    window = reach + TOK_DEV
    padded_keys = jnp.concatenate([jnp.zeros((reach, KV_HEADS, HD), jnp.bfloat16), keys], axis=0)
    padded_values = jnp.concatenate([jnp.zeros((reach, KV_HEADS, HD), jnp.bfloat16), values], axis=0)
    padded_segment = jnp.concatenate([jnp.full((reach,), -1, jnp.int32), segment], axis=0)
    padded_place = jnp.concatenate([jnp.arange(-reach, 0, dtype=jnp.int32), positions], axis=0)
    scale = 1.0 / math.sqrt(HD)

    def one_block(block):
        first = (block * TOK_DEV).astype(jnp.int32)
        query_block = lax.dynamic_slice_in_dim(queries, first, TOK_DEV, 0).reshape(TOK_DEV, TOPK, KV_HEADS, HD)
        key_block = lax.optimization_barrier(lax.dynamic_slice_in_dim(padded_keys, first, window, 0)).astype(jnp.float32)
        value_block = lax.optimization_barrier(lax.dynamic_slice_in_dim(padded_values, first, window, 0)).astype(jnp.float32)
        key_segment = lax.dynamic_slice_in_dim(padded_segment, first, window, 0)
        key_place = lax.dynamic_slice_in_dim(padded_place, first, window, 0)
        query_segment = lax.dynamic_slice_in_dim(segment, first, TOK_DEV, 0)
        query_place = lax.dynamic_slice_in_dim(positions, first, TOK_DEV, 0)
        allowed = (query_segment[:, None] == key_segment[None, :]) & (key_place[None, :] <= query_place[:, None])

        def one_expert(expert_query):
            scores = jnp.einsum('qhd,khd->qhk', expert_query.astype(jnp.float32), key_block) * scale
            masked = jnp.where(allowed[:, None, :], scores, -jnp.inf)
            peak = lax.optimization_barrier(jnp.max(masked, axis=-1, keepdims=True))
            weight = jnp.exp(masked - peak)
            total = lax.optimization_barrier(jnp.sum(weight, axis=-1))
            rounded = lax.optimization_barrier(weight.astype(jnp.bfloat16)).astype(jnp.float32)
            summed = jnp.einsum('qhk,khd->qhd', rounded, value_block)
            return (summed / total[:, :, None]).astype(jnp.bfloat16)
        outputs = lax.map(one_expert, jnp.moveaxis(query_block, 1, 0))
        return jnp.moveaxis(outputs, 0, 1).reshape(TOK_DEV, TOPK, KVW)
    attended = lax.map(one_block, jnp.arange(TOKENS // TOK_DEV, dtype=jnp.int32)).reshape(TOKENS, TOPK, KVW)
    stacked = jnp.stack([keys.reshape(TOKENS, KVW), values.reshape(TOKENS, KVW)], axis=1)
    pages = stacked.reshape(POOL, PAGE, 2, KVW)
    cache = jnp.zeros_like(pages).at[page_table].set(pages)
    return (attended, cache)
```

```python
import math

import jax
import jax.numpy as jnp
from jax import lax
from jax.sharding import PartitionSpec as P

HD = 128
TOPK = 2
PAGE = 16
BACK = 6


def from_behind(value, axis, by):
    peers = lax.axis_size(axis)
    pairs = [(i, i + by) for i in range(peers) if 0 <= i + by < peers]
    return lax.ppermute(value, axis, pairs)


def segment_info(positions, prompt_pages):
    ends = PAGE * jnp.cumsum(prompt_pages)
    below = ends[None, :] <= positions[:, None]
    segment = jnp.sum(below.astype(jnp.int32), axis=1)
    start = jnp.max(jnp.where(below, ends[None, :], 0), axis=1)
    return (segment, positions - start)


def rotate_heads(raw, offsets):
    half = HD // 2
    inverse = 10000.0 ** (-(2.0 * jnp.arange(half, dtype=jnp.float32)) / HD)
    angle = offsets.astype(jnp.float32)[:, None] * inverse[None, :]
    cosine = jnp.cos(angle)[:, None, :]
    sine = jnp.sin(angle)[:, None, :]
    lower = raw[..., :half]
    upper = raw[..., half:]
    return jnp.concatenate([lower * cosine - upper * sine, upper * cosine + lower * sine], axis=-1)


def body(tokens, key_weight, value_weight, queries, prompt_pages, page_table):
    block_rows = tokens.shape[0]
    width = key_weight.shape[1]
    local_heads = width // HD
    devices = lax.axis_size("seq")
    first_row = lax.axis_index("seq") * block_rows
    positions = first_row + jnp.arange(block_rows, dtype=jnp.int32)
    segment, offsets = segment_info(positions, prompt_pages)
    piece = lax.all_gather(tokens, "tp", axis=1, tiled=True)
    raw_keys = jnp.dot(piece, key_weight, preferred_element_type=jnp.float32)
    raw_values = jnp.dot(piece, value_weight, preferred_element_type=jnp.float32)
    keys = rotate_heads(raw_keys.reshape(block_rows, local_heads, HD), offsets).astype(jnp.bfloat16)
    values = raw_values.astype(jnp.bfloat16)
    key_value = jnp.stack([keys.reshape(block_rows, width), values], axis=1)
    blocks = [key_value]
    for distance in range(1, BACK + 1):
        blocks.append(from_behind(key_value, "seq", distance))
    query = queries.reshape(block_rows, TOPK, local_heads, HD)
    scale = 1.0 / math.sqrt(HD)
    masks = []
    for distance in range(BACK + 1):
        key_place = positions - distance * block_rows
        key_segment, unused_offsets = segment_info(key_place, prompt_pages)
        allowed = (segment[:, None] == key_segment[None, :]) & (
            key_place[None, :] <= positions[:, None]
        )
        masks.append(allowed & (key_place[None, :] >= 0))

    def block_scores(expert_query, block, allowed):
        key_heads = block[:, 0].reshape(block_rows, local_heads, HD)
        scores = (
            jnp.einsum("qhd,khd->qhk", expert_query, key_heads, preferred_element_type=jnp.float32)
            * scale
        )
        return jnp.where(allowed[:, None, :], scores, -jnp.inf)

    outputs = []
    for expert in range(TOPK):
        expert_query = query[:, expert]
        score_list = []
        for distance in range(BACK + 1):
            block = blocks[distance]
            allowed = masks[distance]

            def compute(block=block, allowed=allowed):
                return block_scores(expert_query, block, allowed)

            score_list.append(compute())
        peak = jnp.max(score_list[0], axis=-1)
        for distance in range(1, BACK + 1):
            peak = jnp.maximum(peak, jnp.max(score_list[distance], axis=-1))
        total = jnp.zeros((block_rows, local_heads), jnp.float32)
        summed = jnp.zeros((block_rows, local_heads, HD), jnp.float32)
        for distance in range(BACK + 1):
            block = blocks[distance]
            allowed = masks[distance]
            scores = score_list[distance]

            def accumulate(state, block=block, scores=scores):
                weight = jnp.exp(scores - peak[..., None])
                rounded = weight.astype(jnp.bfloat16)
                value_heads = block[:, 1].reshape(block_rows, local_heads, HD)
                product = jnp.einsum(
                    "qhk,khd->qhd", rounded, value_heads, preferred_element_type=jnp.float32
                )
                return (state[0] + jnp.sum(weight, axis=-1), state[1] + product)

            total, summed = accumulate((total, summed))
        outputs.append((summed / total[..., None]).astype(jnp.bfloat16))
    attended = jnp.stack(outputs, axis=1).reshape(block_rows, TOPK, width)
    pages_dev = block_rows // PAGE
    capacity = max(1, pages_dev // devices)
    page_data = key_value.reshape(pages_dev, PAGE * 2 * width)
    owner = page_table // pages_dev
    place_on_owner = page_table % pages_dev
    page_order = jnp.arange(pages_dev, dtype=jnp.int32)
    earlier = (owner[:, None] == owner[None, :]) & (page_order[None, :] < page_order[:, None])
    rank = jnp.sum(earlier.astype(jnp.int32), axis=1)
    target = (owner[None, None, :] == jnp.arange(devices, dtype=jnp.int32)[:, None, None]) & (
        rank[None, None, :] == jnp.arange(capacity, dtype=jnp.int32)[None, :, None]
    )
    outgoing = jnp.einsum(
        "dcp,pf->dcf", target.astype(jnp.bfloat16), page_data, preferred_element_type=jnp.float32
    ).astype(jnp.bfloat16)
    labels = jnp.sum(jnp.where(target, place_on_owner[None, None, :] + 1, 0), axis=2) - 1
    incoming, arrived = (
        lax.all_to_all(outgoing, "seq", split_axis=0, concat_axis=0, tiled=True),
        lax.all_to_all(labels, "seq", split_axis=0, concat_axis=0, tiled=True),
    )
    placing = (arrived.reshape(-1)[None, :] == page_order[:, None]).astype(jnp.bfloat16)
    pool = jnp.dot(
        placing,
        incoming.reshape(devices * capacity, PAGE * 2 * width),
        preferred_element_type=jnp.float32,
    ).astype(jnp.bfloat16)
    cache = pool.reshape(pages_dev, PAGE, 2, width)
    return (attended, cache)


def solution(mesh):
    in_specs = (P("seq", "tp"), P(None, "tp"), P(None, "tp"), P("seq", None, "tp"), P(), P("seq"))
    out_specs = (P("seq", None, "tp"), P("seq", None, None, "tp"))
    return jax.shard_map(body, mesh=mesh, in_specs=in_specs, out_specs=out_specs, check_vma=False)
```

```python
import math

import jax
import jax.numpy as jnp
from jax import lax
from jax.sharding import PartitionSpec as P


HD = 128
TOPK = 2
PAGE = 16
BACK = 6


def from_behind(value, axis, by):
    peers = lax.axis_size(axis)
    pairs = [(i, i + by) for i in range(peers) if 0 <= i + by < peers]
    return lax.ppermute(value, axis, pairs)


def segment_info(positions, prompt_pages):
    ends = PAGE * jnp.cumsum(prompt_pages)
    below = ends[None, :] <= positions[:, None]
    segment = jnp.sum(below.astype(jnp.int32), axis=1)
    start = jnp.max(jnp.where(below, ends[None, :], 0), axis=1)
    return (segment, positions - start)


def rotate_heads(raw, offsets):
    half = HD // 2
    inverse = 10000.0 ** (-(2.0 * jnp.arange(half, dtype=jnp.float32)) / HD)
    angle = offsets.astype(jnp.float32)[:, None] * inverse[None, :]
    cosine = jnp.cos(angle)[:, None, :]
    sine = jnp.sin(angle)[:, None, :]
    lower = raw[..., :half]
    upper = raw[..., half:]
    return jnp.concatenate([lower * cosine - upper * sine, upper * cosine + lower * sine], axis=-1)


def body(tokens, key_weight, value_weight, queries, prompt_pages, page_table):
    block_rows = tokens.shape[0]
    width = key_weight.shape[1]
    local_heads = width // HD
    devices = lax.axis_size("seq")
    first_row = lax.axis_index("seq") * block_rows
    positions = first_row + jnp.arange(block_rows, dtype=jnp.int32)
    segment, offsets = segment_info(positions, prompt_pages)
    piece = lax.all_gather(tokens, "tp", axis=1, tiled=True)
    raw_keys = jnp.dot(piece, key_weight, preferred_element_type=jnp.float32)
    raw_values = jnp.dot(piece, value_weight, preferred_element_type=jnp.float32)
    keys = rotate_heads(raw_keys.reshape(block_rows, local_heads, HD), offsets).astype(jnp.bfloat16)
    values = raw_values.astype(jnp.bfloat16)
    key_value = jnp.stack([keys.reshape(block_rows, width), values], axis=1)
    blocks = [key_value]
    for distance in range(1, BACK + 1):
        blocks.append(from_behind(key_value, "seq", distance))
    query = queries.reshape(block_rows, TOPK, local_heads, HD)
    scale = 1.0 / math.sqrt(HD)
    masks = []
    for distance in range(BACK + 1):
        key_place = positions - distance * block_rows
        key_segment, _ = segment_info(key_place, prompt_pages)
        allowed = (segment[:, None] == key_segment[None, :]) & (
            key_place[None, :] <= positions[:, None]
        )
        masks.append(allowed & (key_place[None, :] >= 0))

    def block_scores(expert_query, block, allowed):
        key_heads = block[:, 0].reshape(block_rows, local_heads, HD)
        scores = (
            jnp.einsum("qhd,khd->qhk", expert_query, key_heads, preferred_element_type=jnp.float32)
            * scale
        )
        return jnp.where(allowed[:, None, :], scores, -jnp.inf)

    outputs = []
    for expert in range(TOPK):
        expert_query = query[:, expert]
        score_list = []
        for distance in range(BACK + 1):
            block = blocks[distance]
            allowed = masks[distance]

            def compute(block=block, allowed=allowed):
                return block_scores(expert_query, block, allowed)

            score_list.append(compute())
        peak = jnp.max(score_list[0], axis=-1)
        for distance in range(1, BACK + 1):
            peak = jnp.maximum(peak, jnp.max(score_list[distance], axis=-1))
        total = jnp.zeros((block_rows, local_heads), jnp.float32)
        summed = jnp.zeros((block_rows, local_heads, HD), jnp.float32)
        for distance in range(BACK + 1):
            block = blocks[distance]
            allowed = masks[distance]
            scores = score_list[distance]

            def accumulate(state, block=block, scores=scores):
                weight = jnp.exp(scores - peak[..., None])
                rounded = weight.astype(jnp.bfloat16)
                value_heads = block[:, 1].reshape(block_rows, local_heads, HD)
                product = jnp.einsum(
                    "qhk,khd->qhd", rounded, value_heads, preferred_element_type=jnp.float32
                )
                return (state[0] + jnp.sum(weight, axis=-1), state[1] + product)

            total, summed = accumulate((total, summed))
        outputs.append((summed / total[..., None]).astype(jnp.bfloat16))
    attended = jnp.stack(outputs, axis=1).reshape(block_rows, TOPK, width)
    pages_dev = block_rows // PAGE
    capacity = max(1, pages_dev // devices)
    owner = page_table // pages_dev
    place_on_owner = page_table % pages_dev
    page_order = jnp.arange(pages_dev, dtype=jnp.int32)
    earlier = (owner[:, None] == owner[None, :]) & (page_order[None, :] < page_order[:, None])
    rank = jnp.sum(earlier.astype(jnp.int32), axis=1)
    target = (owner[None, None, :] == jnp.arange(devices, dtype=jnp.int32)[:, None, None]) & (
        rank[None, None, :] == jnp.arange(capacity, dtype=jnp.int32)[None, :, None]
    )
    pages = key_value.reshape(pages_dev, PAGE, 2, width)
    page_index = jnp.sum(jnp.where(target, page_order[None, None, :], 0), axis=2)
    outgoing = pages[page_index.reshape(-1)]
    labels = jnp.sum(jnp.where(target, place_on_owner[None, None, :] + 1, 0), axis=2) - 1
    incoming = lax.all_to_all(outgoing, "seq", split_axis=0, concat_axis=0, tiled=True)
    arrived = lax.all_to_all(labels, "seq", split_axis=0, concat_axis=0, tiled=True)
    slots = jnp.arange(devices * capacity, dtype=jnp.int32)
    source_slot = jnp.sum(
        jnp.where(arrived.reshape(-1)[None, :] == page_order[:, None], slots[None, :], 0), axis=1
    )
    cache = incoming[source_slot]
    return (attended, cache)


def solution(mesh):
    in_specs = (P("seq", "tp"), P(None, "tp"), P(None, "tp"), P("seq", None, "tp"), P(), P("seq"))
    out_specs = (P("seq", None, "tp"), P("seq", None, None, "tp"))
    return jax.shard_map(body, mesh=mesh, in_specs=in_specs, out_specs=out_specs, check_vma=False)
```

```python
import functools
import math

import jax
import jax.numpy as jnp
from jax import lax
from jax.experimental import pallas as pl
from jax.sharding import PartitionSpec as P


HD = 128
TOPK = 2
PAGE = 16
BACK = 6


def from_behind(value, axis, by):
    peers = lax.axis_size(axis)
    pairs = [(i, i + by) for i in range(peers) if 0 <= i + by < peers]
    return lax.ppermute(value, axis, pairs)


def segment_info(positions, prompt_pages):
    ends = PAGE * jnp.cumsum(prompt_pages)
    below = ends[None, :] <= positions[:, None]
    segment = jnp.sum(below.astype(jnp.int32), axis=1)
    start = jnp.max(jnp.where(below, ends[None, :], 0), axis=1)
    return (segment, positions - start)


def rotate_heads(raw, offsets):
    half = HD // 2
    inverse = 10000.0 ** (-(2.0 * jnp.arange(half, dtype=jnp.float32)) / HD)
    angle = offsets.astype(jnp.float32)[:, None] * inverse[None, :]
    cosine = jnp.cos(angle)[:, None, :]
    sine = jnp.sin(angle)[:, None, :]
    lower = raw[..., :half]
    upper = raw[..., half:]
    return jnp.concatenate([lower * cosine - upper * sine, upper * cosine + lower * sine], axis=-1)


def attention_kernel(query_segment_ref, key_segment_ref, query_ref, *refs, blocks, scale):
    key_refs = refs[:blocks]
    value_refs = refs[blocks : 2 * blocks]
    out_ref = refs[2 * blocks]
    rows = query_ref.shape[0]
    query = query_ref[...]
    query_segment = query_segment_ref[...]
    row = lax.broadcasted_iota(jnp.int32, (rows, rows), 0)
    col = lax.broadcasted_iota(jnp.int32, (rows, rows), 1)

    def scores(distance):
        key = key_refs[distance][...]
        product = lax.dot_general(
            query, key, (((1,), (1,)), ((), ())), preferred_element_type=jnp.float32
        )
        allowed = query_segment == key_segment_ref[pl.ds(distance, 1), :]
        if distance == 0:
            allowed = allowed & (col <= row)
        return jnp.where(allowed, product * scale, -jnp.inf)

    peak = jnp.max(scores(0), axis=1, keepdims=True)
    for distance in range(1, blocks):
        peak = jnp.maximum(peak, jnp.max(scores(distance), axis=1, keepdims=True))
    total = jnp.zeros((rows, 1), jnp.float32)
    summed = jnp.zeros((rows, out_ref.shape[1]), jnp.float32)
    for distance in range(blocks):
        weight = jnp.exp(scores(distance) - peak)
        total = total + jnp.sum(weight, axis=1, keepdims=True)
        summed = summed + jnp.dot(
            weight.astype(jnp.bfloat16),
            value_refs[distance][...],
            preferred_element_type=jnp.float32,
        )
    out_ref[...] = (summed / total).astype(out_ref.dtype)


def attend(query, query_segment, key_segment, blocks_kv, local_heads):
    rows = query.shape[0]
    blocks = len(blocks_kv)
    grid = (local_heads, TOPK)
    query_spec = pl.BlockSpec((rows, HD), lambda h, e: (0, e * local_heads + h))
    key_spec = pl.BlockSpec((rows, HD), lambda h, e: (0, h))
    value_spec = pl.BlockSpec((rows, HD), lambda h, e: (0, local_heads + h))
    in_specs = (
        [
            pl.BlockSpec((rows, 1), lambda h, e: (0, 0)),
            pl.BlockSpec((blocks, rows), lambda h, e: (0, 0)),
            query_spec,
        ]
        + [key_spec] * blocks
        + [value_spec] * blocks
    )
    combos = local_heads * TOPK
    cost = pl.CostEstimate(
        flops=combos * 3 * blocks * 2 * rows * rows * HD,
        transcendentals=combos * blocks * rows * rows,
        bytes_accessed=2 * query.size * 2 + blocks * rows * 2 * local_heads * HD * 2,
    )
    kernel = functools.partial(attention_kernel, blocks=blocks, scale=1.0 / math.sqrt(HD))
    return pl.pallas_call(
        kernel,
        grid=grid,
        in_specs=in_specs,
        out_specs=query_spec,
        out_shape=jax.ShapeDtypeStruct(query.shape, jnp.bfloat16),
        cost_estimate=cost,
        name="block_attention",
    )(query_segment, key_segment, query, *blocks_kv, *blocks_kv)


def body(tokens, key_weight, value_weight, queries, prompt_pages, page_table):
    block_rows = tokens.shape[0]
    width = key_weight.shape[1]
    local_heads = width // HD
    devices = lax.axis_size("seq")
    first_row = lax.axis_index("seq") * block_rows
    positions = first_row + jnp.arange(block_rows, dtype=jnp.int32)
    segment, offsets = segment_info(positions, prompt_pages)
    piece = lax.all_gather(tokens, "tp", axis=1, tiled=True)
    raw_keys = jnp.dot(piece, key_weight, preferred_element_type=jnp.float32)
    raw_values = jnp.dot(piece, value_weight, preferred_element_type=jnp.float32)
    keys = rotate_heads(raw_keys.reshape(block_rows, local_heads, HD), offsets).astype(jnp.bfloat16)
    values = raw_values.astype(jnp.bfloat16)
    key_value = jnp.concatenate([keys.reshape(block_rows, width), values], axis=1)
    blocks = [key_value]
    for distance in range(1, BACK + 1):
        blocks.append(from_behind(key_value, "seq", distance))
    key_place = positions[None, :] - block_rows * jnp.arange(BACK + 1, dtype=jnp.int32)[:, None]
    key_segment, _ = segment_info(key_place.reshape(-1), prompt_pages)
    key_segment = jnp.where(key_place >= 0, key_segment.reshape(BACK + 1, block_rows), -1)
    query = queries.reshape(block_rows, TOPK * width)
    attended = attend(query, segment[:, None], key_segment, blocks, local_heads)
    attended = attended.reshape(block_rows, TOPK, width)
    pages_dev = block_rows // PAGE
    capacity = max(1, pages_dev // devices)
    owner = page_table // pages_dev
    place_on_owner = page_table % pages_dev
    page_order = jnp.arange(pages_dev, dtype=jnp.int32)
    earlier = (owner[:, None] == owner[None, :]) & (page_order[None, :] < page_order[:, None])
    rank = jnp.sum(earlier.astype(jnp.int32), axis=1)
    target = (owner[None, None, :] == jnp.arange(devices, dtype=jnp.int32)[:, None, None]) & (
        rank[None, None, :] == jnp.arange(capacity, dtype=jnp.int32)[None, :, None]
    )
    pages = key_value.reshape(pages_dev, PAGE, 2, width)
    page_index = jnp.sum(jnp.where(target, page_order[None, None, :], 0), axis=2)
    outgoing = pages[page_index.reshape(-1)]
    labels = jnp.sum(jnp.where(target, place_on_owner[None, None, :] + 1, 0), axis=2) - 1
    incoming = lax.all_to_all(outgoing, "seq", split_axis=0, concat_axis=0, tiled=True)
    arrived = lax.all_to_all(labels, "seq", split_axis=0, concat_axis=0, tiled=True)
    slots = jnp.arange(devices * capacity, dtype=jnp.int32)
    source_slot = jnp.sum(
        jnp.where(arrived.reshape(-1)[None, :] == page_order[:, None], slots[None, :], 0), axis=1
    )
    cache = incoming[source_slot]
    return (attended, cache)


def solution(mesh):
    in_specs = (P("seq", "tp"), P(None, "tp"), P(None, "tp"), P("seq", None, "tp"), P(), P("seq"))
    out_specs = (P("seq", None, "tp"), P("seq", None, None, "tp"))
    return jax.shard_map(body, mesh=mesh, in_specs=in_specs, out_specs=out_specs, check_vma=False)
```

```python
import functools
import math

import jax
import jax.numpy as jnp
from jax import lax
from jax.experimental import pallas as pl
from jax.sharding import PartitionSpec as P


HD = 128
TOPK = 2
PAGE = 16
BACK = 6


def from_behind(value, axis, by):
    peers = lax.axis_size(axis)
    pairs = [(i, i + by) for i in range(peers) if 0 <= i + by < peers]
    return lax.ppermute(value, axis, pairs)


def segment_info(positions, prompt_pages):
    ends = PAGE * jnp.cumsum(prompt_pages)
    below = ends[None, :] <= positions[:, None]
    segment = jnp.sum(below.astype(jnp.int32), axis=1)
    start = jnp.max(jnp.where(below, ends[None, :], 0), axis=1)
    return (segment, positions - start)


def rotate_heads(raw, offsets):
    half = HD // 2
    inverse = 10000.0 ** (-(2.0 * jnp.arange(half, dtype=jnp.float32)) / HD)
    angle = offsets.astype(jnp.float32)[:, None] * inverse[None, :]
    cosine = jnp.cos(angle)[:, None, :]
    sine = jnp.sin(angle)[:, None, :]
    lower = raw[..., :half]
    upper = raw[..., half:]
    return jnp.concatenate([lower * cosine - upper * sine, upper * cosine + lower * sine], axis=-1)


def attention_kernel(query_segment_ref, key_segment_ref, query_ref, *refs, blocks, scale):
    key_refs = refs[:blocks]
    value_refs = refs[blocks : 2 * blocks]
    out_ref = refs[2 * blocks]
    rows = query_ref.shape[0]
    query = query_ref[...]
    query_segment = query_segment_ref[...]
    row = lax.broadcasted_iota(jnp.int32, (rows, rows), 0)
    col = lax.broadcasted_iota(jnp.int32, (rows, rows), 1)

    def scores(distance):
        key = key_refs[distance][...]
        product = lax.dot_general(
            query, key, (((1,), (1,)), ((), ())), preferred_element_type=jnp.float32
        )
        allowed = query_segment == key_segment_ref[pl.ds(distance, 1), :]
        if distance == 0:
            allowed = allowed & (col <= row)
        return jnp.where(allowed, product * scale, -jnp.inf)

    peak = jnp.max(scores(0), axis=1, keepdims=True)
    for distance in range(1, blocks):
        peak = jnp.maximum(peak, jnp.max(scores(distance), axis=1, keepdims=True))
    total = jnp.zeros((rows, 1), jnp.float32)
    summed = jnp.zeros((rows, out_ref.shape[1]), jnp.float32)
    for distance in range(blocks):
        weight = jnp.exp(scores(distance) - peak)
        total = total + jnp.sum(weight, axis=1, keepdims=True)
        summed = summed + jnp.dot(
            weight.astype(jnp.bfloat16),
            value_refs[distance][...],
            preferred_element_type=jnp.float32,
        )
    out_ref[...] = (summed / total).astype(out_ref.dtype)


def attend(query, query_segment, key_segment, sources, local_heads):
    rows = query.shape[0]
    blocks = len(sources)
    grid = (local_heads, TOPK)
    query_spec = pl.BlockSpec((rows, HD), lambda h, e: (0, e * local_heads + h))

    def column_spec(base):
        return pl.BlockSpec((rows, HD), lambda h, e: (0, base + h))

    key_specs = [column_spec(base) for _, base in sources]
    value_specs = [column_spec(base + local_heads) for _, base in sources]
    in_specs = (
        [
            pl.BlockSpec((rows, 1), lambda h, e: (0, 0)),
            pl.BlockSpec((blocks, rows), lambda h, e: (0, 0)),
            query_spec,
        ]
        + key_specs
        + value_specs
    )
    arrays = [array for array, _ in sources]
    combos = local_heads * TOPK
    cost = pl.CostEstimate(
        flops=combos * 3 * blocks * 2 * rows * rows * HD,
        transcendentals=combos * blocks * rows * rows,
        bytes_accessed=2 * query.size * 2 + blocks * rows * 2 * local_heads * HD * 2,
    )
    kernel = functools.partial(attention_kernel, blocks=blocks, scale=1.0 / math.sqrt(HD))
    return pl.pallas_call(
        kernel,
        grid=grid,
        in_specs=in_specs,
        out_specs=query_spec,
        out_shape=jax.ShapeDtypeStruct(query.shape, jnp.bfloat16),
        cost_estimate=cost,
        name="block_attention",
    )(query_segment, key_segment, query, *arrays, *arrays)


def body(tokens, key_weight, value_weight, queries, prompt_pages, page_table):
    block_rows = tokens.shape[0]
    width = key_weight.shape[1]
    local_heads = width // HD
    devices = lax.axis_size("seq")
    first_row = lax.axis_index("seq") * block_rows
    positions = first_row + jnp.arange(block_rows, dtype=jnp.int32)
    segment, offsets = segment_info(positions, prompt_pages)
    piece = lax.all_gather(tokens, "tp", axis=1, tiled=True)
    raw_keys = jnp.dot(piece, key_weight, preferred_element_type=jnp.float32)
    raw_values = jnp.dot(piece, value_weight, preferred_element_type=jnp.float32)
    keys = rotate_heads(raw_keys.reshape(block_rows, local_heads, HD), offsets).astype(jnp.bfloat16)
    values = raw_values.astype(jnp.bfloat16)
    key_value = jnp.concatenate([keys.reshape(block_rows, width), values], axis=1)
    odd = [from_behind(key_value, "seq", distance) for distance in range(1, BACK + 1, 2)]
    even = from_behind(jnp.concatenate(odd, axis=1), "seq", 1)
    span = 2 * local_heads
    sources = [(key_value, 0)]
    for distance in range(1, BACK + 1):
        if distance % 2:
            sources.append((odd[distance // 2], 0))
        else:
            sources.append((even, span * (distance // 2 - 1)))
    key_place = positions[None, :] - block_rows * jnp.arange(BACK + 1, dtype=jnp.int32)[:, None]
    key_segment, _ = segment_info(key_place.reshape(-1), prompt_pages)
    key_segment = jnp.where(key_place >= 0, key_segment.reshape(BACK + 1, block_rows), -1)
    query = queries.reshape(block_rows, TOPK * width)
    attended = attend(query, segment[:, None], key_segment, sources, local_heads)
    attended = attended.reshape(block_rows, TOPK, width)
    pages_dev = block_rows // PAGE
    capacity = max(1, pages_dev // devices)
    owner = page_table // pages_dev
    place_on_owner = page_table % pages_dev
    page_order = jnp.arange(pages_dev, dtype=jnp.int32)
    earlier = (owner[:, None] == owner[None, :]) & (page_order[None, :] < page_order[:, None])
    rank = jnp.sum(earlier.astype(jnp.int32), axis=1)
    target = (owner[None, None, :] == jnp.arange(devices, dtype=jnp.int32)[:, None, None]) & (
        rank[None, None, :] == jnp.arange(capacity, dtype=jnp.int32)[None, :, None]
    )
    pages = key_value.reshape(pages_dev, PAGE, 2, width)
    page_index = jnp.sum(jnp.where(target, page_order[None, None, :], 0), axis=2)
    outgoing = pages[page_index.reshape(-1)]
    labels = jnp.sum(jnp.where(target, place_on_owner[None, None, :] + 1, 0), axis=2) - 1
    incoming = lax.all_to_all(outgoing, "seq", split_axis=0, concat_axis=0, tiled=True)
    arrived = lax.all_to_all(labels, "seq", split_axis=0, concat_axis=0, tiled=True)
    slots = jnp.arange(devices * capacity, dtype=jnp.int32)
    source_slot = jnp.sum(
        jnp.where(arrived.reshape(-1)[None, :] == page_order[:, None], slots[None, :], 0), axis=1
    )
    cache = incoming[source_slot]
    return (attended, cache)


def solution(mesh):
    in_specs = (P("seq", "tp"), P(None, "tp"), P(None, "tp"), P("seq", None, "tp"), P(), P("seq"))
    out_specs = (P("seq", None, "tp"), P("seq", None, None, "tp"))
    return jax.shard_map(body, mesh=mesh, in_specs=in_specs, out_specs=out_specs, check_vma=False)
```

```python
import functools
import math

import jax
import jax.numpy as jnp
from jax import lax
from jax.experimental import pallas as pl
from jax.sharding import PartitionSpec as P


HD = 128
TOPK = 2
PAGE = 16
BACK = 6


def from_behind(value, axis, by):
    peers = lax.axis_size(axis)
    pairs = [(i, i + by) for i in range(peers) if 0 <= i + by < peers]
    return lax.ppermute(value, axis, pairs)


def segment_info(positions, prompt_pages):
    ends = PAGE * jnp.cumsum(prompt_pages)
    below = ends[None, :] <= positions[:, None]
    segment = jnp.sum(below.astype(jnp.int32), axis=1)
    start = jnp.max(jnp.where(below, ends[None, :], 0), axis=1)
    return (segment, positions - start)


def rotate_heads(raw, offsets):
    half = HD // 2
    inverse = 10000.0 ** (-(2.0 * jnp.arange(half, dtype=jnp.float32)) / HD)
    angle = offsets.astype(jnp.float32)[:, None] * inverse[None, :]
    cosine = jnp.cos(angle)[:, None, :]
    sine = jnp.sin(angle)[:, None, :]
    lower = raw[..., :half]
    upper = raw[..., half:]
    return jnp.concatenate([lower * cosine - upper * sine, upper * cosine + lower * sine], axis=-1)


def attention_kernel(query_segment_ref, key_segment_ref, query_ref, *refs, blocks, scale):
    key_refs = refs[:blocks]
    value_refs = refs[blocks : 2 * blocks]
    out_ref = refs[2 * blocks]
    rows = query_ref.shape[0]
    query = query_ref[...]
    query_segment = query_segment_ref[...]
    row = lax.broadcasted_iota(jnp.int32, (rows, rows), 0)
    col = lax.broadcasted_iota(jnp.int32, (rows, rows), 1)

    def scores(distance):
        key = key_refs[distance][...]
        product = lax.dot_general(
            query, key, (((1,), (1,)), ((), ())), preferred_element_type=jnp.float32
        )
        allowed = query_segment == key_segment_ref[pl.ds(distance, 1), :]
        if distance == 0:
            allowed = allowed & (col <= row)
        return jnp.where(allowed, product * scale, -jnp.inf)

    peak = jnp.max(scores(0), axis=1, keepdims=True)
    for distance in range(1, blocks):
        peak = jnp.maximum(peak, jnp.max(scores(distance), axis=1, keepdims=True))
    total = jnp.zeros((rows, 1), jnp.float32)
    summed = jnp.zeros((rows, out_ref.shape[1]), jnp.float32)
    for distance in range(blocks):
        weight = jnp.exp(scores(distance) - peak)
        total = total + jnp.sum(weight, axis=1, keepdims=True)
        summed = summed + jnp.dot(
            weight.astype(jnp.bfloat16),
            value_refs[distance][...],
            preferred_element_type=jnp.float32,
        )
    out_ref[...] = (summed / total).astype(out_ref.dtype)


def attend(query, query_segment, key_segment, sources, local_heads):
    rows = query.shape[0]
    blocks = len(sources)
    grid = (local_heads, TOPK)
    query_spec = pl.BlockSpec((rows, HD), lambda h, e: (0, e * local_heads + h))

    def column_spec(base):
        return pl.BlockSpec((rows, HD), lambda h, e: (0, base + h))

    key_specs = [column_spec(base) for _, base in sources]
    value_specs = [column_spec(base + local_heads) for _, base in sources]
    in_specs = (
        [
            pl.BlockSpec((rows, 1), lambda h, e: (0, 0)),
            pl.BlockSpec((blocks, rows), lambda h, e: (0, 0)),
            query_spec,
        ]
        + key_specs
        + value_specs
    )
    arrays = [array for array, _ in sources]
    combos = local_heads * TOPK
    cost = pl.CostEstimate(
        flops=combos * 3 * blocks * 2 * rows * rows * HD,
        transcendentals=combos * blocks * rows * rows,
        bytes_accessed=2 * query.size * 2 + blocks * rows * 2 * local_heads * HD * 2,
    )
    kernel = functools.partial(attention_kernel, blocks=blocks, scale=1.0 / math.sqrt(HD))
    return pl.pallas_call(
        kernel,
        grid=grid,
        in_specs=in_specs,
        out_specs=query_spec,
        out_shape=jax.ShapeDtypeStruct(query.shape, jnp.bfloat16),
        cost_estimate=cost,
        name="block_attention",
    )(query_segment, key_segment, query, *arrays, *arrays)


def body(tokens, key_weight, value_weight, queries, prompt_pages, page_table):
    block_rows = tokens.shape[0]
    width = key_weight.shape[1]
    local_heads = width // HD
    devices = lax.axis_size("seq")
    first_row = lax.axis_index("seq") * block_rows
    positions = first_row + jnp.arange(block_rows, dtype=jnp.int32)
    segment, offsets = segment_info(positions, prompt_pages)
    piece = lax.all_gather(tokens, "tp", axis=1, tiled=True)
    raw_keys = jnp.dot(piece, key_weight, preferred_element_type=jnp.float32)
    raw_values = jnp.dot(piece, value_weight, preferred_element_type=jnp.float32)
    keys = rotate_heads(raw_keys.reshape(block_rows, local_heads, HD), offsets).astype(jnp.bfloat16)
    values = raw_values.astype(jnp.bfloat16)
    key_value = jnp.concatenate([keys.reshape(block_rows, width), values], axis=1)
    direct = (1, 3, 5, 6)
    sent = {distance: from_behind(key_value, "seq", distance) for distance in direct}
    relayed = [distance for distance in range(2, BACK + 1) if distance not in direct]
    onward = from_behind(
        jnp.concatenate([sent[distance - 1] for distance in relayed], axis=1), "seq", 1
    )
    span = 2 * local_heads
    sources = [(key_value, 0)]
    for distance in range(1, BACK + 1):
        if distance in sent:
            sources.append((sent[distance], 0))
        else:
            sources.append((onward, span * relayed.index(distance)))
    key_place = positions[None, :] - block_rows * jnp.arange(BACK + 1, dtype=jnp.int32)[:, None]
    key_segment, _ = segment_info(key_place.reshape(-1), prompt_pages)
    key_segment = jnp.where(key_place >= 0, key_segment.reshape(BACK + 1, block_rows), -1)
    query = queries.reshape(block_rows, TOPK * width)
    attended = attend(query, segment[:, None], key_segment, sources, local_heads)
    attended = attended.reshape(block_rows, TOPK, width)
    pages_dev = block_rows // PAGE
    capacity = max(1, pages_dev // devices)
    owner = page_table // pages_dev
    place_on_owner = page_table % pages_dev
    page_order = jnp.arange(pages_dev, dtype=jnp.int32)
    earlier = (owner[:, None] == owner[None, :]) & (page_order[None, :] < page_order[:, None])
    rank = jnp.sum(earlier.astype(jnp.int32), axis=1)
    target = (owner[None, None, :] == jnp.arange(devices, dtype=jnp.int32)[:, None, None]) & (
        rank[None, None, :] == jnp.arange(capacity, dtype=jnp.int32)[None, :, None]
    )
    pages = key_value.reshape(pages_dev, PAGE, 2, width)
    page_index = jnp.sum(jnp.where(target, page_order[None, None, :], 0), axis=2)
    outgoing = pages[page_index.reshape(-1)]
    labels = jnp.sum(jnp.where(target, place_on_owner[None, None, :] + 1, 0), axis=2) - 1
    incoming = lax.all_to_all(outgoing, "seq", split_axis=0, concat_axis=0, tiled=True)
    arrived = lax.all_to_all(labels, "seq", split_axis=0, concat_axis=0, tiled=True)
    slots = jnp.arange(devices * capacity, dtype=jnp.int32)
    source_slot = jnp.sum(
        jnp.where(arrived.reshape(-1)[None, :] == page_order[:, None], slots[None, :], 0), axis=1
    )
    cache = incoming[source_slot]
    return (attended, cache)


def solution(mesh):
    in_specs = (P("seq", "tp"), P(None, "tp"), P(None, "tp"), P("seq", None, "tp"), P(), P("seq"))
    out_specs = (P("seq", None, "tp"), P("seq", None, None, "tp"))
    return jax.shard_map(body, mesh=mesh, in_specs=in_specs, out_specs=out_specs, check_vma=False)
```

```python
import functools
import math

import jax
import jax.numpy as jnp
from jax import lax
from jax.experimental import pallas as pl
from jax.sharding import PartitionSpec as P


HD = 128
TOPK = 2
PAGE = 16
BACK = 6


def from_behind(value, axis, by):
    peers = lax.axis_size(axis)
    pairs = [(i, i + by) for i in range(peers) if 0 <= i + by < peers]
    return lax.ppermute(value, axis, pairs)


def segment_info(positions, prompt_pages):
    ends = PAGE * jnp.cumsum(prompt_pages)
    below = ends[None, :] <= positions[:, None]
    segment = jnp.sum(below.astype(jnp.int32), axis=1)
    start = jnp.max(jnp.where(below, ends[None, :], 0), axis=1)
    return (segment, positions - start)


def rotate_heads(raw, offsets):
    half = HD // 2
    inverse = 10000.0 ** (-(2.0 * jnp.arange(half, dtype=jnp.float32)) / HD)
    angle = offsets.astype(jnp.float32)[:, None] * inverse[None, :]
    cosine = jnp.cos(angle)[:, None, :]
    sine = jnp.sin(angle)[:, None, :]
    lower = raw[..., :half]
    upper = raw[..., half:]
    return jnp.concatenate([lower * cosine - upper * sine, upper * cosine + lower * sine], axis=-1)


def attention_kernel(query_segment_ref, key_segment_ref, query_ref, *refs, blocks, scale):
    key_refs = refs[:blocks]
    value_refs = refs[blocks : 2 * blocks]
    out_ref = refs[2 * blocks]
    rows = query_ref.shape[0]
    query = query_ref[...]
    query_segment = query_segment_ref[...]
    row = lax.broadcasted_iota(jnp.int32, (rows, rows), 0)
    col = lax.broadcasted_iota(jnp.int32, (rows, rows), 1)

    def scores(distance):
        key = key_refs[distance][...]
        product = lax.dot_general(
            query, key, (((1,), (1,)), ((), ())), preferred_element_type=jnp.float32
        )
        allowed = query_segment == key_segment_ref[pl.ds(distance, 1), :]
        if distance == 0:
            allowed = allowed & (col <= row)
        return jnp.where(allowed, product * scale, -jnp.inf)

    peak = jnp.max(scores(0), axis=1, keepdims=True)
    for distance in range(1, blocks):
        peak = jnp.maximum(peak, jnp.max(scores(distance), axis=1, keepdims=True))
    total = jnp.zeros((rows, 1), jnp.float32)
    summed = jnp.zeros((rows, out_ref.shape[1]), jnp.float32)
    for distance in range(blocks):
        weight = jnp.exp(scores(distance) - peak)
        total = total + jnp.sum(weight, axis=1, keepdims=True)
        summed = summed + jnp.dot(
            weight.astype(jnp.bfloat16),
            value_refs[distance][...],
            preferred_element_type=jnp.float32,
        )
    out_ref[...] = (summed / total).astype(out_ref.dtype)


def attend(query, query_segment, key_segment, sources, local_heads):
    rows = query.shape[0]
    blocks = len(sources)
    grid = (local_heads, TOPK)
    query_spec = pl.BlockSpec((rows, HD), lambda h, e: (0, e * local_heads + h))

    def column_spec(base):
        return pl.BlockSpec((rows, HD), lambda h, e: (0, base + h))

    key_specs = [column_spec(base) for _, base in sources]
    value_specs = [column_spec(base + local_heads) for _, base in sources]
    in_specs = (
        [
            pl.BlockSpec((rows, 1), lambda h, e: (0, 0)),
            pl.BlockSpec((blocks, rows), lambda h, e: (0, 0)),
            query_spec,
        ]
        + key_specs
        + value_specs
    )
    arrays = [array for array, _ in sources]
    combos = local_heads * TOPK
    cost = pl.CostEstimate(
        flops=combos * 3 * blocks * 2 * rows * rows * HD,
        transcendentals=combos * blocks * rows * rows,
        bytes_accessed=2 * query.size * 2 + blocks * rows * 2 * local_heads * HD * 2,
    )
    kernel = functools.partial(attention_kernel, blocks=blocks, scale=1.0 / math.sqrt(HD))
    return pl.pallas_call(
        kernel,
        grid=grid,
        in_specs=in_specs,
        out_specs=query_spec,
        out_shape=jax.ShapeDtypeStruct(query.shape, jnp.bfloat16),
        cost_estimate=cost,
        name="block_attention",
    )(query_segment, key_segment, query, *arrays, *arrays)


def body(tokens, key_weight, value_weight, queries, prompt_pages, page_table):
    block_rows = tokens.shape[0]
    width = key_weight.shape[1]
    local_heads = width // HD
    devices = lax.axis_size("seq")
    first_row = lax.axis_index("seq") * block_rows
    positions = first_row + jnp.arange(block_rows, dtype=jnp.int32)
    segment, offsets = segment_info(positions, prompt_pages)
    own = tokens.reshape(block_rows, 1, 1, tokens.shape[1])
    across = lax.all_gather(own, "zhi", axis=1, tiled=True)
    piece = lax.all_gather(across, "core", axis=2, tiled=True).reshape(block_rows, -1)
    raw_keys = jnp.dot(piece, key_weight, preferred_element_type=jnp.float32)
    raw_values = jnp.dot(piece, value_weight, preferred_element_type=jnp.float32)
    keys = rotate_heads(raw_keys.reshape(block_rows, local_heads, HD), offsets).astype(jnp.bfloat16)
    values = raw_values.astype(jnp.bfloat16)
    key_value = jnp.concatenate([keys.reshape(block_rows, width), values], axis=1)
    direct = (1, 3, 5, 6)
    sent = {distance: from_behind(key_value, "seq", distance) for distance in direct}
    relayed = [distance for distance in range(2, BACK + 1) if distance not in direct]
    onward = from_behind(
        jnp.concatenate([sent[distance - 1] for distance in relayed], axis=1), "seq", 1
    )
    span = 2 * local_heads
    sources = [(key_value, 0)]
    for distance in range(1, BACK + 1):
        if distance in sent:
            sources.append((sent[distance], 0))
        else:
            sources.append((onward, span * relayed.index(distance)))
    key_place = positions[None, :] - block_rows * jnp.arange(BACK + 1, dtype=jnp.int32)[:, None]
    key_segment, _ = segment_info(key_place.reshape(-1), prompt_pages)
    key_segment = jnp.where(key_place >= 0, key_segment.reshape(BACK + 1, block_rows), -1)
    query = queries.reshape(block_rows, TOPK * width)
    attended = attend(query, segment[:, None], key_segment, sources, local_heads)
    attended = attended.reshape(block_rows, TOPK, width)
    pages_dev = block_rows // PAGE
    capacity = max(1, pages_dev // devices)
    owner = page_table // pages_dev
    place_on_owner = page_table % pages_dev
    page_order = jnp.arange(pages_dev, dtype=jnp.int32)
    earlier = (owner[:, None] == owner[None, :]) & (page_order[None, :] < page_order[:, None])
    rank = jnp.sum(earlier.astype(jnp.int32), axis=1)
    target = (owner[None, None, :] == jnp.arange(devices, dtype=jnp.int32)[:, None, None]) & (
        rank[None, None, :] == jnp.arange(capacity, dtype=jnp.int32)[None, :, None]
    )
    pages = key_value.reshape(pages_dev, PAGE, 2, width)
    page_index = jnp.sum(jnp.where(target, page_order[None, None, :], 0), axis=2)
    outgoing = pages[page_index.reshape(-1)]
    labels = jnp.sum(jnp.where(target, place_on_owner[None, None, :] + 1, 0), axis=2) - 1
    incoming = lax.all_to_all(outgoing, "seq", split_axis=0, concat_axis=0, tiled=True)
    arrived = lax.all_to_all(labels, "seq", split_axis=0, concat_axis=0, tiled=True)
    slots = jnp.arange(devices * capacity, dtype=jnp.int32)
    source_slot = jnp.sum(
        jnp.where(arrived.reshape(-1)[None, :] == page_order[:, None], slots[None, :], 0), axis=1
    )
    cache = incoming[source_slot]
    return (attended, cache)


def solution(mesh):
    seq, tp = mesh.devices.shape
    chips = jax.sharding.Mesh(mesh.devices.reshape(seq, tp // 2, 2), ("seq", "zhi", "core"))
    heads = ("zhi", "core")
    in_specs = (P("seq", heads), P(None, heads), P(None, heads), P("seq", None, heads), P(), P("seq"))
    out_specs = (P("seq", None, heads), P("seq", None, None, heads))
    return jax.shard_map(body, mesh=chips, in_specs=in_specs, out_specs=out_specs, check_vma=False)
```

```python
import functools
import math

import jax
import jax.numpy as jnp
from jax import lax
from jax.experimental import pallas as pl
from jax.sharding import PartitionSpec as P


HD = 128
TOPK = 2
PAGE = 16
BACK = 6


def from_behind(value, axis, by):
    peers = lax.axis_size(axis)
    pairs = [(i, i + by) for i in range(peers) if 0 <= i + by < peers]
    return lax.ppermute(value, axis, pairs)


def segment_info(positions, prompt_pages):
    ends = PAGE * jnp.cumsum(prompt_pages)
    below = ends[None, :] <= positions[:, None]
    segment = jnp.sum(below.astype(jnp.int32), axis=1)
    start = jnp.max(jnp.where(below, ends[None, :], 0), axis=1)
    return (segment, positions - start)


def rotate_heads(raw, offsets):
    half = HD // 2
    inverse = 10000.0 ** (-(2.0 * jnp.arange(half, dtype=jnp.float32)) / HD)
    angle = offsets.astype(jnp.float32)[:, None] * inverse[None, :]
    cosine = jnp.cos(angle)[:, None, :]
    sine = jnp.sin(angle)[:, None, :]
    lower = raw[..., :half]
    upper = raw[..., half:]
    return jnp.concatenate([lower * cosine - upper * sine, upper * cosine + lower * sine], axis=-1)


def masked_scores(query, query_segment, key_segment_ref, key_ref, slot, diagonal, scale):
    rows = query.shape[0]
    product = lax.dot_general(
        query, key_ref[...], (((1,), (1,)), ((), ())), preferred_element_type=jnp.float32
    )
    allowed = query_segment == key_segment_ref[pl.ds(slot, 1), :]
    if diagonal:
        row = lax.broadcasted_iota(jnp.int32, (rows, rows), 0)
        col = lax.broadcasted_iota(jnp.int32, (rows, rows), 1)
        allowed = allowed & (col <= row)
    return jnp.where(allowed, product * scale, -jnp.inf)


def accumulate(scores, value_refs, peak, total, summed):
    for slot, value_ref in enumerate(value_refs):
        weight = jnp.exp(scores(slot) - peak)
        total = total + jnp.sum(weight, axis=1, keepdims=True)
        summed = summed + jnp.dot(
            weight.astype(jnp.bfloat16), value_ref[...], preferred_element_type=jnp.float32
        )
    return total, summed


def first_kernel(query_segment_ref, key_segment_ref, query_ref, *refs, blocks, scale):
    key_refs = refs[:blocks]
    value_refs = refs[blocks : 2 * blocks]
    peak_ref, total_ref, summed_ref = refs[2 * blocks :]
    query = query_ref[...]
    query_segment = query_segment_ref[...]

    def scores(slot):
        return masked_scores(
            query, query_segment, key_segment_ref, key_refs[slot], slot, slot == 0, scale
        )

    peak = jnp.max(scores(0), axis=1, keepdims=True)
    for slot in range(1, blocks):
        peak = jnp.maximum(peak, jnp.max(scores(slot), axis=1, keepdims=True))
    total = jnp.zeros(peak.shape, jnp.float32)
    summed = jnp.zeros(summed_ref.shape, jnp.float32)
    total, summed = accumulate(scores, value_refs, peak, total, summed)
    peak_ref[...] = jnp.broadcast_to(peak, peak_ref.shape)
    total_ref[...] = jnp.broadcast_to(total, total_ref.shape)
    summed_ref[...] = summed


def second_kernel(
    query_segment_ref, key_segment_ref, query_ref, peak_ref, total_ref, summed_ref, *refs,
    blocks, scale,
):
    key_refs = refs[:blocks]
    value_refs = refs[blocks : 2 * blocks]
    out_ref = refs[2 * blocks]
    query = query_ref[...]
    query_segment = query_segment_ref[...]

    def scores(slot):
        return masked_scores(
            query, query_segment, key_segment_ref, key_refs[slot], slot, False, scale
        )

    first_peak = peak_ref[:, :1]
    peak = first_peak
    for slot in range(blocks):
        peak = jnp.maximum(peak, jnp.max(scores(slot), axis=1, keepdims=True))
    factor = jnp.exp(first_peak - peak)
    total = total_ref[:, :1] * factor
    summed = summed_ref[...] * factor
    total, summed = accumulate(scores, value_refs, peak, total, summed)
    out_ref[...] = (summed / total).astype(out_ref.dtype)


def attend(query, query_segment, key_segment, first, second, local_heads):
    rows = query.shape[0]
    grid = (local_heads, TOPK)
    combos = local_heads * TOPK
    scale = 1.0 / math.sqrt(HD)
    tile = pl.BlockSpec((rows, HD), lambda h, e: (0, e * local_heads + h))

    def column_spec(base):
        return pl.BlockSpec((rows, HD), lambda h, e: (0, base + h))

    def common(sources):
        specs = [
            pl.BlockSpec((rows, 1), lambda h, e: (0, 0)),
            pl.BlockSpec((len(sources), rows), lambda h, e: (0, 0)),
            tile,
        ]
        return specs

    def block_specs(sources):
        keys = [column_spec(base) for _, base in sources]
        values = [column_spec(base + local_heads) for _, base in sources]
        arrays = [array for array, _ in sources]
        return keys + values, arrays + arrays

    def cost(blocks):
        return pl.CostEstimate(
            flops=combos * 3 * blocks * 2 * rows * rows * HD,
            transcendentals=combos * blocks * rows * rows,
            bytes_accessed=query.size * 2 + blocks * rows * 2 * local_heads * HD * 2
            + 3 * combos * rows * HD * 4,
        )

    stats = jax.ShapeDtypeStruct((rows, combos * HD), jnp.float32)
    specs, arrays = block_specs(first)
    peak, total, summed = pl.pallas_call(
        functools.partial(first_kernel, blocks=len(first), scale=scale),
        grid=grid,
        in_specs=common(first) + specs,
        out_specs=(tile, tile, tile),
        out_shape=(stats, stats, stats),
        cost_estimate=cost(len(first)),
        name="first_blocks",
    )(query_segment, key_segment[0], query, *arrays)
    specs, arrays = block_specs(second)
    return pl.pallas_call(
        functools.partial(second_kernel, blocks=len(second), scale=scale),
        grid=grid,
        in_specs=common(second) + [tile, tile, tile] + specs,
        out_specs=tile,
        out_shape=jax.ShapeDtypeStruct(query.shape, jnp.bfloat16),
        cost_estimate=cost(len(second)),
        name="second_blocks",
    )(query_segment, key_segment[1], query, peak, total, summed, *arrays)


def body(tokens, key_weight, value_weight, queries, prompt_pages, page_table):
    block_rows = tokens.shape[0]
    width = key_weight.shape[1]
    local_heads = width // HD
    devices = lax.axis_size("seq")
    first_row = lax.axis_index("seq") * block_rows
    positions = first_row + jnp.arange(block_rows, dtype=jnp.int32)
    segment, offsets = segment_info(positions, prompt_pages)
    piece = lax.all_gather(tokens, "tp", axis=1, tiled=True)
    raw_keys = jnp.dot(piece, key_weight, preferred_element_type=jnp.float32)
    raw_values = jnp.dot(piece, value_weight, preferred_element_type=jnp.float32)
    keys = rotate_heads(raw_keys.reshape(block_rows, local_heads, HD), offsets).astype(jnp.bfloat16)
    values = raw_values.astype(jnp.bfloat16)
    key_value = jnp.concatenate([keys.reshape(block_rows, width), values], axis=1)
    direct = (1, 3, 5, 6)
    sent = {distance: from_behind(key_value, "seq", distance) for distance in direct}
    relayed = [distance for distance in range(2, BACK + 1) if distance not in direct]
    onward = from_behind(
        jnp.concatenate([sent[distance - 1] for distance in relayed], axis=1), "seq", 1
    )
    span = 2 * local_heads
    first = [(key_value, 0)] + [(sent[distance], 0) for distance in direct]
    second = [(onward, span * index) for index in range(len(relayed))]
    order = [0] + list(direct) + relayed
    key_place = positions[None, :] - block_rows * jnp.asarray(order, jnp.int32)[:, None]
    key_segment, _ = segment_info(key_place.reshape(-1), prompt_pages)
    key_segment = jnp.where(key_place >= 0, key_segment.reshape(len(order), block_rows), -1)
    key_segment = (key_segment[: len(first)], key_segment[len(first) :])
    query = queries.reshape(block_rows, TOPK * width)
    attended = attend(query, segment[:, None], key_segment, first, second, local_heads)
    attended = attended.reshape(block_rows, TOPK, width)
    pages_dev = block_rows // PAGE
    capacity = max(1, pages_dev // devices)
    owner = page_table // pages_dev
    place_on_owner = page_table % pages_dev
    page_order = jnp.arange(pages_dev, dtype=jnp.int32)
    earlier = (owner[:, None] == owner[None, :]) & (page_order[None, :] < page_order[:, None])
    rank = jnp.sum(earlier.astype(jnp.int32), axis=1)
    target = (owner[None, None, :] == jnp.arange(devices, dtype=jnp.int32)[:, None, None]) & (
        rank[None, None, :] == jnp.arange(capacity, dtype=jnp.int32)[None, :, None]
    )
    pages = key_value.reshape(pages_dev, PAGE, 2, width)
    page_index = jnp.sum(jnp.where(target, page_order[None, None, :], 0), axis=2)
    outgoing = pages[page_index.reshape(-1)]
    labels = jnp.sum(jnp.where(target, place_on_owner[None, None, :] + 1, 0), axis=2) - 1
    incoming = lax.all_to_all(outgoing, "seq", split_axis=0, concat_axis=0, tiled=True)
    arrived = lax.all_to_all(labels, "seq", split_axis=0, concat_axis=0, tiled=True)
    slots = jnp.arange(devices * capacity, dtype=jnp.int32)
    source_slot = jnp.sum(
        jnp.where(arrived.reshape(-1)[None, :] == page_order[:, None], slots[None, :], 0), axis=1
    )
    cache = incoming[source_slot]
    return (attended, cache)


def solution(mesh):
    in_specs = (P("seq", "tp"), P(None, "tp"), P(None, "tp"), P("seq", None, "tp"), P(), P("seq"))
    out_specs = (P("seq", None, "tp"), P("seq", None, None, "tp"))
    return jax.shard_map(body, mesh=mesh, in_specs=in_specs, out_specs=out_specs, check_vma=False)
```

```python
import functools
import math

import jax
import jax.numpy as jnp
from jax import lax
from jax.experimental import pallas as pl
from jax.experimental.pallas import tpu as pltpu
from jax.sharding import PartitionSpec as P


HD = 128
TOPK = 2
PAGE = 16
BACK = 6


def from_behind(value, axis, by):
    peers = lax.axis_size(axis)
    pairs = [(i, i + by) for i in range(peers) if 0 <= i + by < peers]
    return lax.ppermute(value, axis, pairs)


def segment_info(positions, prompt_pages):
    ends = PAGE * jnp.cumsum(prompt_pages)
    below = ends[None, :] <= positions[:, None]
    segment = jnp.sum(below.astype(jnp.int32), axis=1)
    start = jnp.max(jnp.where(below, ends[None, :], 0), axis=1)
    return (segment, positions - start)


def project_kernel(piece_ref, key_weight_ref, value_weight_ref, cosine_ref, sine_ref, out_ref):
    piece = piece_ref[...]
    width = key_weight_ref.shape[1]
    keys = jnp.dot(piece, key_weight_ref[...], preferred_element_type=jnp.float32)
    values = jnp.dot(piece, value_weight_ref[...], preferred_element_type=jnp.float32)
    cosine = cosine_ref[...]
    sine = sine_ref[...]
    for head in range(width // HD):
        raw = keys[:, head * HD : (head + 1) * HD]
        turned = raw * cosine + pltpu.roll(raw, HD // 2, 1) * sine
        out_ref[:, head * HD : (head + 1) * HD] = turned.astype(out_ref.dtype)
    out_ref[:, width:] = values.astype(out_ref.dtype)


def project(piece, key_weight, value_weight, offsets):
    rows = piece.shape[0]
    width = key_weight.shape[1]
    half = HD // 2
    inverse = 10000.0 ** (-(2.0 * jnp.arange(half, dtype=jnp.float32)) / HD)
    angle = offsets.astype(jnp.float32)[:, None] * inverse[None, :]
    cosine = jnp.cos(angle)
    sine = jnp.sin(angle)
    cosine = jnp.concatenate([cosine, cosine], axis=1)
    sine = jnp.concatenate([-sine, sine], axis=1)
    cost = pl.CostEstimate(
        flops=2 * 2 * rows * piece.shape[1] * width,
        transcendentals=0,
        bytes_accessed=piece.size * 2 + 2 * key_weight.size * 2 + rows * 2 * width * 2,
    )
    return pl.pallas_call(
        project_kernel,
        out_shape=jax.ShapeDtypeStruct((rows, 2 * width), jnp.bfloat16),
        cost_estimate=cost,
        name="project_rotate",
    )(piece, key_weight, value_weight, cosine, sine)


def masked_scores(query, query_segment, key_segment_ref, key_ref, slot, diagonal, scale):
    rows = query.shape[0]
    product = lax.dot_general(
        query, key_ref[...], (((1,), (1,)), ((), ())), preferred_element_type=jnp.float32
    )
    allowed = query_segment == key_segment_ref[pl.ds(slot, 1), :]
    if diagonal:
        row = lax.broadcasted_iota(jnp.int32, (rows, rows), 0)
        col = lax.broadcasted_iota(jnp.int32, (rows, rows), 1)
        allowed = allowed & (col <= row)
    return jnp.where(allowed, product * scale, -jnp.inf)


def accumulate(scores, value_refs, peak, total, summed):
    for slot, value_ref in enumerate(value_refs):
        weight = jnp.exp(scores(slot) - peak)
        total = total + jnp.sum(weight, axis=1, keepdims=True)
        summed = summed + jnp.dot(
            weight.astype(jnp.bfloat16), value_ref[...], preferred_element_type=jnp.float32
        )
    return total, summed


def first_kernel(query_segment_ref, key_segment_ref, query_ref, *refs, blocks, scale):
    key_refs = refs[:blocks]
    value_refs = refs[blocks : 2 * blocks]
    peak_ref, total_ref, summed_ref = refs[2 * blocks :]
    query = query_ref[...]
    query_segment = query_segment_ref[...]

    def scores(slot):
        return masked_scores(
            query, query_segment, key_segment_ref, key_refs[slot], slot, slot == 0, scale
        )

    peak = jnp.max(scores(0), axis=1, keepdims=True)
    for slot in range(1, blocks):
        peak = jnp.maximum(peak, jnp.max(scores(slot), axis=1, keepdims=True))
    total = jnp.zeros(peak.shape, jnp.float32)
    summed = jnp.zeros(summed_ref.shape, jnp.float32)
    total, summed = accumulate(scores, value_refs, peak, total, summed)
    peak_ref[...] = jnp.broadcast_to(peak, peak_ref.shape)
    total_ref[...] = jnp.broadcast_to(total, total_ref.shape)
    summed_ref[...] = summed


def second_kernel(
    query_segment_ref, key_segment_ref, query_ref, peak_ref, total_ref, summed_ref, *refs,
    blocks, scale,
):
    key_refs = refs[:blocks]
    value_refs = refs[blocks : 2 * blocks]
    out_ref = refs[2 * blocks]
    query = query_ref[...]
    query_segment = query_segment_ref[...]

    def scores(slot):
        return masked_scores(
            query, query_segment, key_segment_ref, key_refs[slot], slot, False, scale
        )

    first_peak = peak_ref[:, :1]
    peak = first_peak
    for slot in range(blocks):
        peak = jnp.maximum(peak, jnp.max(scores(slot), axis=1, keepdims=True))
    factor = jnp.exp(first_peak - peak)
    total = total_ref[:, :1] * factor
    summed = summed_ref[...] * factor
    total, summed = accumulate(scores, value_refs, peak, total, summed)
    out_ref[...] = (summed / total).astype(out_ref.dtype)


def attend(query, query_segment, key_segment, first, second, local_heads):
    rows = query.shape[0]
    grid = (local_heads, TOPK)
    combos = local_heads * TOPK
    scale = 1.0 / math.sqrt(HD)
    tile = pl.BlockSpec((rows, HD), lambda h, e: (0, e * local_heads + h))

    def column_spec(base):
        return pl.BlockSpec((rows, HD), lambda h, e: (0, base + h))

    def common(sources):
        specs = [
            pl.BlockSpec((rows, 1), lambda h, e: (0, 0)),
            pl.BlockSpec((len(sources), rows), lambda h, e: (0, 0)),
            tile,
        ]
        return specs

    def block_specs(sources):
        keys = [column_spec(base) for _, base in sources]
        values = [column_spec(base + local_heads) for _, base in sources]
        arrays = [array for array, _ in sources]
        return keys + values, arrays + arrays

    def cost(blocks):
        return pl.CostEstimate(
            flops=combos * 3 * blocks * 2 * rows * rows * HD,
            transcendentals=combos * blocks * rows * rows,
            bytes_accessed=query.size * 2 + blocks * rows * 2 * local_heads * HD * 2
            + 3 * combos * rows * HD * 4,
        )

    stats = jax.ShapeDtypeStruct((rows, combos * HD), jnp.float32)
    specs, arrays = block_specs(first)
    peak, total, summed = pl.pallas_call(
        functools.partial(first_kernel, blocks=len(first), scale=scale),
        grid=grid,
        in_specs=common(first) + specs,
        out_specs=(tile, tile, tile),
        out_shape=(stats, stats, stats),
        cost_estimate=cost(len(first)),
        name="first_blocks",
    )(query_segment, key_segment[0], query, *arrays)
    specs, arrays = block_specs(second)
    return pl.pallas_call(
        functools.partial(second_kernel, blocks=len(second), scale=scale),
        grid=grid,
        in_specs=common(second) + [tile, tile, tile] + specs,
        out_specs=tile,
        out_shape=jax.ShapeDtypeStruct(query.shape, jnp.bfloat16),
        cost_estimate=cost(len(second)),
        name="second_blocks",
    )(query_segment, key_segment[1], query, peak, total, summed, *arrays)


def body(tokens, key_weight, value_weight, queries, prompt_pages, page_table):
    block_rows = tokens.shape[0]
    width = key_weight.shape[1]
    local_heads = width // HD
    devices = lax.axis_size("seq")
    first_row = lax.axis_index("seq") * block_rows
    positions = first_row + jnp.arange(block_rows, dtype=jnp.int32)
    segment, offsets = segment_info(positions, prompt_pages)
    piece = lax.all_gather(tokens, "tp", axis=1, tiled=True)
    key_value = project(piece, key_weight, value_weight, offsets)
    direct = (1, 3, 5, 6)
    sent = {distance: from_behind(key_value, "seq", distance) for distance in direct}
    relayed = [distance for distance in range(2, BACK + 1) if distance not in direct]
    onward = from_behind(
        jnp.concatenate([sent[distance - 1] for distance in relayed], axis=1), "seq", 1
    )
    span = 2 * local_heads
    first = [(key_value, 0)] + [(sent[distance], 0) for distance in direct]
    second = [(onward, span * index) for index in range(len(relayed))]
    order = [0] + list(direct) + relayed
    key_place = positions[None, :] - block_rows * jnp.asarray(order, jnp.int32)[:, None]
    key_segment, _ = segment_info(key_place.reshape(-1), prompt_pages)
    key_segment = jnp.where(key_place >= 0, key_segment.reshape(len(order), block_rows), -1)
    key_segment = (key_segment[: len(first)], key_segment[len(first) :])
    query = queries.reshape(block_rows, TOPK * width)
    attended = attend(query, segment[:, None], key_segment, first, second, local_heads)
    attended = attended.reshape(block_rows, TOPK, width)
    pages_dev = block_rows // PAGE
    capacity = max(1, pages_dev // devices)
    owner = page_table // pages_dev
    place_on_owner = page_table % pages_dev
    page_order = jnp.arange(pages_dev, dtype=jnp.int32)
    earlier = (owner[:, None] == owner[None, :]) & (page_order[None, :] < page_order[:, None])
    rank = jnp.sum(earlier.astype(jnp.int32), axis=1)
    target = (owner[None, None, :] == jnp.arange(devices, dtype=jnp.int32)[:, None, None]) & (
        rank[None, None, :] == jnp.arange(capacity, dtype=jnp.int32)[None, :, None]
    )
    pages = key_value.reshape(pages_dev, PAGE, 2, width)
    page_index = jnp.sum(jnp.where(target, page_order[None, None, :], 0), axis=2)
    outgoing = pages[page_index.reshape(-1)]
    labels = jnp.sum(jnp.where(target, place_on_owner[None, None, :] + 1, 0), axis=2) - 1
    incoming = lax.all_to_all(outgoing, "seq", split_axis=0, concat_axis=0, tiled=True)
    arrived = lax.all_to_all(labels, "seq", split_axis=0, concat_axis=0, tiled=True)
    slots = jnp.arange(devices * capacity, dtype=jnp.int32)
    source_slot = jnp.sum(
        jnp.where(arrived.reshape(-1)[None, :] == page_order[:, None], slots[None, :], 0), axis=1
    )
    cache = incoming[source_slot]
    return (attended, cache)


def solution(mesh):
    in_specs = (P("seq", "tp"), P(None, "tp"), P(None, "tp"), P("seq", None, "tp"), P(), P("seq"))
    out_specs = (P("seq", None, "tp"), P("seq", None, None, "tp"))
    return jax.shard_map(body, mesh=mesh, in_specs=in_specs, out_specs=out_specs, check_vma=False)
```

```python
import functools
import math

import jax
import jax.numpy as jnp
from jax import lax
from jax.experimental import pallas as pl
from jax.experimental.pallas import tpu as pltpu
from jax.sharding import PartitionSpec as P


HD = 128
TOPK = 2
PAGE = 16
BACK = 6


def from_behind(value, axis, by):
    peers = lax.axis_size(axis)
    pairs = [(i, i + by) for i in range(peers) if 0 <= i + by < peers]
    return lax.ppermute(value, axis, pairs)


def segment_info(positions, prompt_pages):
    ends = PAGE * jnp.cumsum(prompt_pages)
    below = ends[None, :] <= positions[:, None]
    segment = jnp.sum(below.astype(jnp.int32), axis=1)
    start = jnp.max(jnp.where(below, ends[None, :], 0), axis=1)
    return (segment, positions - start)


def project_kernel(piece_ref, key_weight_ref, value_weight_ref, cosine_ref, sine_ref, out_ref):
    rows = out_ref.shape[0]
    width = key_weight_ref.shape[1]
    share = piece_ref.shape[1]
    keys = jnp.zeros((rows, width), jnp.float32)
    values = jnp.zeros((rows, width), jnp.float32)
    for part in range(piece_ref.shape[0] // rows):
        chunk = piece_ref[part * rows : (part + 1) * rows, :]
        keys = keys + jnp.dot(
            chunk, key_weight_ref[part * share : (part + 1) * share, :],
            preferred_element_type=jnp.float32,
        )
        values = values + jnp.dot(
            chunk, value_weight_ref[part * share : (part + 1) * share, :],
            preferred_element_type=jnp.float32,
        )
    cosine = cosine_ref[...]
    sine = sine_ref[...]
    for head in range(width // HD):
        raw = keys[:, head * HD : (head + 1) * HD]
        turned = raw * cosine + pltpu.roll(raw, HD // 2, 1) * sine
        out_ref[:, head * HD : (head + 1) * HD] = turned.astype(out_ref.dtype)
    out_ref[:, width:] = values.astype(out_ref.dtype)


def project(piece, key_weight, value_weight, offsets):
    rows = offsets.shape[0]
    width = key_weight.shape[1]
    half = HD // 2
    inverse = 10000.0 ** (-(2.0 * jnp.arange(half, dtype=jnp.float32)) / HD)
    angle = offsets.astype(jnp.float32)[:, None] * inverse[None, :]
    cosine = jnp.cos(angle)
    sine = jnp.sin(angle)
    cosine = jnp.concatenate([cosine, cosine], axis=1)
    sine = jnp.concatenate([-sine, sine], axis=1)
    cost = pl.CostEstimate(
        flops=2 * 2 * rows * key_weight.shape[0] * width,
        transcendentals=0,
        bytes_accessed=piece.size * 2 + 2 * key_weight.size * 2 + rows * 2 * width * 2,
    )
    return pl.pallas_call(
        project_kernel,
        out_shape=jax.ShapeDtypeStruct((rows, 2 * width), jnp.bfloat16),
        cost_estimate=cost,
        name="project_rotate",
    )(piece, key_weight, value_weight, cosine, sine)


def masked_scores(query, query_segment, key_segment_ref, key_ref, slot, diagonal, scale):
    rows = query.shape[0]
    product = lax.dot_general(
        query, key_ref[...], (((1,), (1,)), ((), ())), preferred_element_type=jnp.float32
    )
    allowed = query_segment == key_segment_ref[pl.ds(slot, 1), :]
    if diagonal:
        row = lax.broadcasted_iota(jnp.int32, (rows, rows), 0)
        col = lax.broadcasted_iota(jnp.int32, (rows, rows), 1)
        allowed = allowed & (col <= row)
    return jnp.where(allowed, product * scale, -jnp.inf)


def accumulate(scores, value_refs, peak, total, summed):
    for slot, value_ref in enumerate(value_refs):
        weight = jnp.exp(scores(slot) - peak)
        total = total + jnp.sum(weight, axis=1, keepdims=True)
        summed = summed + jnp.dot(
            weight.astype(jnp.bfloat16), value_ref[...], preferred_element_type=jnp.float32
        )
    return total, summed


def first_kernel(query_segment_ref, key_segment_ref, query_ref, *refs, blocks, scale):
    key_refs = refs[:blocks]
    value_refs = refs[blocks : 2 * blocks]
    peak_ref, total_ref, summed_ref = refs[2 * blocks :]
    query = query_ref[...]
    query_segment = query_segment_ref[...]

    def scores(slot):
        return masked_scores(
            query, query_segment, key_segment_ref, key_refs[slot], slot, slot == 0, scale
        )

    peak = jnp.max(scores(0), axis=1, keepdims=True)
    for slot in range(1, blocks):
        peak = jnp.maximum(peak, jnp.max(scores(slot), axis=1, keepdims=True))
    total = jnp.zeros(peak.shape, jnp.float32)
    summed = jnp.zeros(summed_ref.shape, jnp.float32)
    total, summed = accumulate(scores, value_refs, peak, total, summed)
    peak_ref[...] = jnp.broadcast_to(peak, peak_ref.shape)
    total_ref[...] = jnp.broadcast_to(total, total_ref.shape)
    summed_ref[...] = summed


def second_kernel(
    query_segment_ref, key_segment_ref, query_ref, peak_ref, total_ref, summed_ref, *refs,
    blocks, scale,
):
    key_refs = refs[:blocks]
    value_refs = refs[blocks : 2 * blocks]
    out_ref = refs[2 * blocks]
    query = query_ref[...]
    query_segment = query_segment_ref[...]

    def scores(slot):
        return masked_scores(
            query, query_segment, key_segment_ref, key_refs[slot], slot, False, scale
        )

    first_peak = peak_ref[:, :1]
    peak = first_peak
    for slot in range(blocks):
        peak = jnp.maximum(peak, jnp.max(scores(slot), axis=1, keepdims=True))
    factor = jnp.exp(first_peak - peak)
    total = total_ref[:, :1] * factor
    summed = summed_ref[...] * factor
    total, summed = accumulate(scores, value_refs, peak, total, summed)
    out_ref[...] = (summed / total).astype(out_ref.dtype)


def attend(query, query_segment, key_segment, first, second, local_heads):
    rows = query.shape[0]
    grid = (local_heads, TOPK)
    combos = local_heads * TOPK
    scale = 1.0 / math.sqrt(HD)
    tile = pl.BlockSpec((rows, HD), lambda h, e: (0, e * local_heads + h))

    def column_spec(base):
        return pl.BlockSpec((rows, HD), lambda h, e: (0, base + h))

    def common(sources):
        specs = [
            pl.BlockSpec((rows, 1), lambda h, e: (0, 0)),
            pl.BlockSpec((len(sources), rows), lambda h, e: (0, 0)),
            tile,
        ]
        return specs

    def block_specs(sources):
        keys = [column_spec(base) for _, base in sources]
        values = [column_spec(base + local_heads) for _, base in sources]
        arrays = [array for array, _ in sources]
        return keys + values, arrays + arrays

    def cost(blocks):
        return pl.CostEstimate(
            flops=combos * 3 * blocks * 2 * rows * rows * HD,
            transcendentals=combos * blocks * rows * rows,
            bytes_accessed=query.size * 2 + blocks * rows * 2 * local_heads * HD * 2
            + 3 * combos * rows * HD * 4,
        )

    stats = jax.ShapeDtypeStruct((rows, combos * HD), jnp.float32)
    specs, arrays = block_specs(first)
    peak, total, summed = pl.pallas_call(
        functools.partial(first_kernel, blocks=len(first), scale=scale),
        grid=grid,
        in_specs=common(first) + specs,
        out_specs=(tile, tile, tile),
        out_shape=(stats, stats, stats),
        cost_estimate=cost(len(first)),
        name="first_blocks",
    )(query_segment, key_segment[0], query, *arrays)
    specs, arrays = block_specs(second)
    return pl.pallas_call(
        functools.partial(second_kernel, blocks=len(second), scale=scale),
        grid=grid,
        in_specs=common(second) + [tile, tile, tile] + specs,
        out_specs=tile,
        out_shape=jax.ShapeDtypeStruct(query.shape, jnp.bfloat16),
        cost_estimate=cost(len(second)),
        name="second_blocks",
    )(query_segment, key_segment[1], query, peak, total, summed, *arrays)


def body(tokens, key_weight, value_weight, queries, prompt_pages, page_table):
    block_rows = tokens.shape[0]
    width = key_weight.shape[1]
    local_heads = width // HD
    devices = lax.axis_size("seq")
    first_row = lax.axis_index("seq") * block_rows
    positions = first_row + jnp.arange(block_rows, dtype=jnp.int32)
    segment, offsets = segment_info(positions, prompt_pages)
    piece = lax.all_gather(tokens, "tp", axis=0, tiled=True)
    key_value = project(piece, key_weight, value_weight, offsets)
    direct = (1, 3, 5, 6)
    sent = {distance: from_behind(key_value, "seq", distance) for distance in direct}
    relayed = [distance for distance in range(2, BACK + 1) if distance not in direct]
    onward = from_behind(
        jnp.concatenate([sent[distance - 1] for distance in relayed], axis=1), "seq", 1
    )
    span = 2 * local_heads
    first = [(key_value, 0)] + [(sent[distance], 0) for distance in direct]
    second = [(onward, span * index) for index in range(len(relayed))]
    order = [0] + list(direct) + relayed
    key_place = positions[None, :] - block_rows * jnp.asarray(order, jnp.int32)[:, None]
    key_segment, _ = segment_info(key_place.reshape(-1), prompt_pages)
    key_segment = jnp.where(key_place >= 0, key_segment.reshape(len(order), block_rows), -1)
    key_segment = (key_segment[: len(first)], key_segment[len(first) :])
    query = queries.reshape(block_rows, TOPK * width)
    attended = attend(query, segment[:, None], key_segment, first, second, local_heads)
    attended = attended.reshape(block_rows, TOPK, width)
    pages_dev = block_rows // PAGE
    capacity = max(1, pages_dev // devices)
    owner = page_table // pages_dev
    place_on_owner = page_table % pages_dev
    page_order = jnp.arange(pages_dev, dtype=jnp.int32)
    earlier = (owner[:, None] == owner[None, :]) & (page_order[None, :] < page_order[:, None])
    rank = jnp.sum(earlier.astype(jnp.int32), axis=1)
    target = (owner[None, None, :] == jnp.arange(devices, dtype=jnp.int32)[:, None, None]) & (
        rank[None, None, :] == jnp.arange(capacity, dtype=jnp.int32)[None, :, None]
    )
    pages = key_value.reshape(pages_dev, PAGE, 2, width)
    page_index = jnp.sum(jnp.where(target, page_order[None, None, :], 0), axis=2)
    outgoing = pages[page_index.reshape(-1)]
    labels = jnp.sum(jnp.where(target, place_on_owner[None, None, :] + 1, 0), axis=2) - 1
    incoming = lax.all_to_all(outgoing, "seq", split_axis=0, concat_axis=0, tiled=True)
    arrived = lax.all_to_all(labels, "seq", split_axis=0, concat_axis=0, tiled=True)
    slots = jnp.arange(devices * capacity, dtype=jnp.int32)
    source_slot = jnp.sum(
        jnp.where(arrived.reshape(-1)[None, :] == page_order[:, None], slots[None, :], 0), axis=1
    )
    cache = incoming[source_slot]
    return (attended, cache)


def solution(mesh):
    in_specs = (P("seq", "tp"), P(None, "tp"), P(None, "tp"), P("seq", None, "tp"), P(), P("seq"))
    out_specs = (P("seq", None, "tp"), P("seq", None, None, "tp"))
    return jax.shard_map(body, mesh=mesh, in_specs=in_specs, out_specs=out_specs, check_vma=False)
```

```python
import functools
import math

import jax
import jax.numpy as jnp
from jax import lax
from jax.experimental import pallas as pl
from jax.experimental.pallas import tpu as pltpu
from jax.sharding import PartitionSpec as P


HD = 128
TOPK = 2
PAGE = 16
BACK = 6


def from_behind(value, axis, by):
    peers = lax.axis_size(axis)
    pairs = [(i, i + by) for i in range(peers) if 0 <= i + by < peers]
    return lax.ppermute(value, axis, pairs)


def segment_info(positions, prompt_pages):
    ends = PAGE * jnp.cumsum(prompt_pages)
    below = ends[None, :] <= positions[:, None]
    segment = jnp.sum(below.astype(jnp.int32), axis=1)
    start = jnp.max(jnp.where(below, ends[None, :], 0), axis=1)
    return (segment, positions - start)


def project_kernel(piece_ref, key_weight_ref, value_weight_ref, cosine_ref, sine_ref, out_ref):
    rows = out_ref.shape[0]
    width = key_weight_ref.shape[1]
    share = piece_ref.shape[1]
    keys = jnp.zeros((rows, width), jnp.float32)
    values = jnp.zeros((rows, width), jnp.float32)
    for part in range(piece_ref.shape[0] // rows):
        chunk = piece_ref[part * rows : (part + 1) * rows, :]
        keys = keys + jnp.dot(
            chunk, key_weight_ref[part * share : (part + 1) * share, :],
            preferred_element_type=jnp.float32,
        )
        values = values + jnp.dot(
            chunk, value_weight_ref[part * share : (part + 1) * share, :],
            preferred_element_type=jnp.float32,
        )
    cosine = cosine_ref[...]
    sine = sine_ref[...]
    for head in range(width // HD):
        raw = keys[:, head * HD : (head + 1) * HD]
        turned = raw * cosine + pltpu.roll(raw, HD // 2, 1) * sine
        out_ref[:, head * HD : (head + 1) * HD] = turned.astype(out_ref.dtype)
    out_ref[:, width:] = values.astype(out_ref.dtype)


def project(piece, key_weight, value_weight, offsets):
    rows = offsets.shape[0]
    width = key_weight.shape[1]
    half = HD // 2
    inverse = 10000.0 ** (-(2.0 * jnp.arange(half, dtype=jnp.float32)) / HD)
    angle = offsets.astype(jnp.float32)[:, None] * inverse[None, :]
    cosine = jnp.cos(angle)
    sine = jnp.sin(angle)
    cosine = jnp.concatenate([cosine, cosine], axis=1)
    sine = jnp.concatenate([-sine, sine], axis=1)
    cost = pl.CostEstimate(
        flops=2 * 2 * rows * key_weight.shape[0] * width,
        transcendentals=0,
        bytes_accessed=piece.size * 2 + 2 * key_weight.size * 2 + rows * 2 * width * 2,
    )
    return pl.pallas_call(
        project_kernel,
        out_shape=jax.ShapeDtypeStruct((rows, 2 * width), jnp.bfloat16),
        cost_estimate=cost,
        name="project_rotate",
    )(piece, key_weight, value_weight, cosine, sine)


def masked_scores(query, query_segment, key_segment_ref, key_ref, slot, diagonal, scale):
    rows = query.shape[0]
    product = lax.dot_general(
        query, key_ref[...], (((1,), (1,)), ((), ())), preferred_element_type=jnp.float32
    )
    allowed = query_segment == key_segment_ref[pl.ds(slot, 1), :]
    if diagonal:
        row = lax.broadcasted_iota(jnp.int32, (rows, rows), 0)
        col = lax.broadcasted_iota(jnp.int32, (rows, rows), 1)
        allowed = allowed & (col <= row)
    return jnp.where(allowed, product * scale, -jnp.inf)


def accumulate(scores, value_refs, peak, total, summed):
    for slot, value_ref in enumerate(value_refs):
        weight = jnp.exp(scores(slot) - peak)
        total = total + jnp.sum(weight, axis=1, keepdims=True)
        summed = summed + jnp.dot(
            weight.astype(jnp.bfloat16), value_ref[...], preferred_element_type=jnp.float32
        )
    return total, summed


def first_kernel(query_segment_ref, key_segment_ref, query_ref, *refs, blocks, scale):
    key_refs = refs[:blocks]
    value_refs = refs[blocks : 2 * blocks]
    peak_ref, total_ref, summed_ref = refs[2 * blocks :]
    query = query_ref[...]
    query_segment = query_segment_ref[...]

    def scores(slot):
        return masked_scores(
            query, query_segment, key_segment_ref, key_refs[slot], slot, slot == 0, scale
        )

    peak = jnp.max(scores(0), axis=1, keepdims=True)
    for slot in range(1, blocks):
        peak = jnp.maximum(peak, jnp.max(scores(slot), axis=1, keepdims=True))
    total = jnp.zeros(peak.shape, jnp.float32)
    summed = jnp.zeros(summed_ref.shape, jnp.float32)
    total, summed = accumulate(scores, value_refs, peak, total, summed)
    peak_ref[...] = jnp.broadcast_to(peak, peak_ref.shape)
    total_ref[...] = jnp.broadcast_to(total, total_ref.shape)
    summed_ref[...] = summed


def second_kernel(
    query_segment_ref, key_segment_ref, query_ref, peak_ref, total_ref, summed_ref, *refs,
    blocks, scale,
):
    key_refs = refs[:blocks]
    value_refs = refs[blocks : 2 * blocks]
    out_ref = refs[2 * blocks]
    query = query_ref[...]
    query_segment = query_segment_ref[...]

    def scores(slot):
        return masked_scores(
            query, query_segment, key_segment_ref, key_refs[slot], slot, False, scale
        )

    first_peak = peak_ref[:, :1]
    peak = first_peak
    for slot in range(blocks):
        peak = jnp.maximum(peak, jnp.max(scores(slot), axis=1, keepdims=True))
    factor = jnp.exp(first_peak - peak)
    total = total_ref[:, :1] * factor
    summed = summed_ref[...] * factor
    total, summed = accumulate(scores, value_refs, peak, total, summed)
    out_ref[...] = (summed / total).astype(out_ref.dtype)


def attend(query, query_segment, key_segment, first, second, local_heads):
    rows = query.shape[0]
    grid = (local_heads, TOPK)
    combos = local_heads * TOPK
    scale = 1.0 / math.sqrt(HD)
    tile = pl.BlockSpec((rows, HD), lambda h, e: (0, e * local_heads + h))

    def column_spec(base):
        return pl.BlockSpec((rows, HD), lambda h, e: (0, base + h))

    def common(sources):
        specs = [
            pl.BlockSpec((rows, 1), lambda h, e: (0, 0)),
            pl.BlockSpec((len(sources), rows), lambda h, e: (0, 0)),
            tile,
        ]
        return specs

    def block_specs(sources):
        keys = [column_spec(base) for _, base in sources]
        values = [column_spec(base + local_heads) for _, base in sources]
        arrays = [array for array, _ in sources]
        return keys + values, arrays + arrays

    def cost(blocks):
        return pl.CostEstimate(
            flops=combos * 3 * blocks * 2 * rows * rows * HD,
            transcendentals=combos * blocks * rows * rows,
            bytes_accessed=query.size * 2 + blocks * rows * 2 * local_heads * HD * 2
            + 3 * combos * rows * HD * 4,
        )

    stats = jax.ShapeDtypeStruct((rows, combos * HD), jnp.float32)
    specs, arrays = block_specs(first)
    peak, total, summed = pl.pallas_call(
        functools.partial(first_kernel, blocks=len(first), scale=scale),
        grid=grid,
        in_specs=common(first) + specs,
        out_specs=(tile, tile, tile),
        out_shape=(stats, stats, stats),
        cost_estimate=cost(len(first)),
        name="first_blocks",
    )(query_segment, key_segment[0], query, *arrays)
    specs, arrays = block_specs(second)
    return pl.pallas_call(
        functools.partial(second_kernel, blocks=len(second), scale=scale),
        grid=grid,
        in_specs=common(second) + [tile, tile, tile] + specs,
        out_specs=tile,
        out_shape=jax.ShapeDtypeStruct(query.shape, jnp.bfloat16),
        cost_estimate=cost(len(second)),
        name="second_blocks",
    )(query_segment, key_segment[1], query, peak, total, summed, *arrays)


def body(tokens, key_weight, value_weight, queries, prompt_pages, page_table):
    block_rows = tokens.shape[0]
    width = key_weight.shape[1]
    local_heads = width // HD
    devices = lax.axis_size("seq")
    first_row = lax.axis_index("seq") * block_rows
    positions = first_row + jnp.arange(block_rows, dtype=jnp.int32)
    segment, offsets = segment_info(positions, prompt_pages)
    piece = lax.all_gather(tokens, "tp", axis=0, tiled=True)
    key_value = project(piece, key_weight, value_weight, offsets)
    near, far = (1, 3), (5, 6)
    direct = near + far
    sent = {}
    for distance in near:
        sent[distance] = from_behind(key_value, "seq", distance)
    for distance in far:
        sent[distance] = from_behind(key_value, "seq", distance)
    relayed = [distance for distance in range(2, BACK + 1) if distance not in direct]
    onward = from_behind(
        jnp.concatenate([sent[distance - 1] for distance in relayed], axis=1), "seq", 1
    )
    span = 2 * local_heads
    first = [(key_value, 0)] + [(sent[distance], 0) for distance in direct]
    second = [(onward, span * index) for index in range(len(relayed))]
    order = [0] + list(direct) + relayed
    key_place = positions[None, :] - block_rows * jnp.asarray(order, jnp.int32)[:, None]
    key_segment, _ = segment_info(key_place.reshape(-1), prompt_pages)
    key_segment = jnp.where(key_place >= 0, key_segment.reshape(len(order), block_rows), -1)
    key_segment = (key_segment[: len(first)], key_segment[len(first) :])
    query = queries.reshape(block_rows, TOPK * width)
    attended = attend(query, segment[:, None], key_segment, first, second, local_heads)
    attended = attended.reshape(block_rows, TOPK, width)
    pages_dev = block_rows // PAGE
    capacity = max(1, pages_dev // devices)
    owner = page_table // pages_dev
    place_on_owner = page_table % pages_dev
    page_order = jnp.arange(pages_dev, dtype=jnp.int32)
    earlier = (owner[:, None] == owner[None, :]) & (page_order[None, :] < page_order[:, None])
    rank = jnp.sum(earlier.astype(jnp.int32), axis=1)
    target = (owner[None, None, :] == jnp.arange(devices, dtype=jnp.int32)[:, None, None]) & (
        rank[None, None, :] == jnp.arange(capacity, dtype=jnp.int32)[None, :, None]
    )
    pages = key_value.reshape(pages_dev, PAGE, 2, width)
    page_index = jnp.sum(jnp.where(target, page_order[None, None, :], 0), axis=2)
    outgoing = pages[page_index.reshape(-1)]
    labels = jnp.sum(jnp.where(target, place_on_owner[None, None, :] + 1, 0), axis=2) - 1
    incoming = lax.all_to_all(outgoing, "seq", split_axis=0, concat_axis=0, tiled=True)
    arrived = lax.all_to_all(labels, "seq", split_axis=0, concat_axis=0, tiled=True)
    slots = jnp.arange(devices * capacity, dtype=jnp.int32)
    source_slot = jnp.sum(
        jnp.where(arrived.reshape(-1)[None, :] == page_order[:, None], slots[None, :], 0), axis=1
    )
    cache = incoming[source_slot]
    return (attended, cache)


def solution(mesh):
    in_specs = (P("seq", "tp"), P(None, "tp"), P(None, "tp"), P("seq", None, "tp"), P(), P("seq"))
    out_specs = (P("seq", None, "tp"), P("seq", None, None, "tp"))
    return jax.shard_map(body, mesh=mesh, in_specs=in_specs, out_specs=out_specs, check_vma=False)
```

```python
import functools
import math

import jax
import jax.numpy as jnp
from jax import lax
from jax.experimental import pallas as pl
from jax.experimental.pallas import tpu as pltpu
from jax.sharding import PartitionSpec as P


HD = 128
TOPK = 2
PAGE = 16
BACK = 6


def from_behind(value, axis, by):
    peers = lax.axis_size(axis)
    pairs = [(i, i + by) for i in range(peers) if 0 <= i + by < peers]
    return lax.ppermute(value, axis, pairs)


def segment_info(positions, prompt_pages):
    ends = PAGE * jnp.cumsum(prompt_pages)
    below = ends[None, :] <= positions[:, None]
    segment = jnp.sum(below.astype(jnp.int32), axis=1)
    start = jnp.max(jnp.where(below, ends[None, :], 0), axis=1)
    return (segment, positions - start)


def project_kernel(piece_ref, key_weight_ref, value_weight_ref, cosine_ref, sine_ref, out_ref):
    rows = out_ref.shape[0]
    width = key_weight_ref.shape[1]
    share = piece_ref.shape[1]
    keys = jnp.zeros((rows, width), jnp.float32)
    values = jnp.zeros((rows, width), jnp.float32)
    for part in range(piece_ref.shape[0] // rows):
        chunk = piece_ref[part * rows : (part + 1) * rows, :]
        keys = keys + jnp.dot(
            chunk, key_weight_ref[part * share : (part + 1) * share, :],
            preferred_element_type=jnp.float32,
        )
        values = values + jnp.dot(
            chunk, value_weight_ref[part * share : (part + 1) * share, :],
            preferred_element_type=jnp.float32,
        )
    cosine = cosine_ref[...]
    sine = sine_ref[...]
    for head in range(width // HD):
        raw = keys[:, head * HD : (head + 1) * HD]
        turned = raw * cosine + pltpu.roll(raw, HD // 2, 1) * sine
        out_ref[:, head * HD : (head + 1) * HD] = turned.astype(out_ref.dtype)
    out_ref[:, width:] = values.astype(out_ref.dtype)


def project(piece, key_weight, value_weight, offsets):
    rows = offsets.shape[0]
    width = key_weight.shape[1]
    half = HD // 2
    inverse = 10000.0 ** (-(2.0 * jnp.arange(half, dtype=jnp.float32)) / HD)
    angle = offsets.astype(jnp.float32)[:, None] * inverse[None, :]
    cosine = jnp.cos(angle)
    sine = jnp.sin(angle)
    cosine = jnp.concatenate([cosine, cosine], axis=1)
    sine = jnp.concatenate([-sine, sine], axis=1)
    cost = pl.CostEstimate(
        flops=2 * 2 * rows * key_weight.shape[0] * width,
        transcendentals=0,
        bytes_accessed=piece.size * 2 + 2 * key_weight.size * 2 + rows * 2 * width * 2,
    )
    return pl.pallas_call(
        project_kernel,
        out_shape=jax.ShapeDtypeStruct((rows, 2 * width), jnp.bfloat16),
        cost_estimate=cost,
        name="project_rotate",
    )(piece, key_weight, value_weight, cosine, sine)


def masked_scores(query, query_segment, key_segment_ref, key_ref, slot, diagonal, scale):
    rows = query.shape[0]
    product = lax.dot_general(
        query, key_ref[...], (((1,), (1,)), ((), ())), preferred_element_type=jnp.float32
    )
    allowed = query_segment == key_segment_ref[pl.ds(slot, 1), :]
    if diagonal:
        row = lax.broadcasted_iota(jnp.int32, (rows, rows), 0)
        col = lax.broadcasted_iota(jnp.int32, (rows, rows), 1)
        allowed = allowed & (col <= row)
    return jnp.where(allowed, product * scale, -jnp.inf)


def accumulate(scores, value_refs, peak, total, summed):
    for slot, value_ref in enumerate(value_refs):
        weight = jnp.exp(scores(slot) - peak)
        total = total + jnp.sum(weight, axis=1, keepdims=True)
        summed = summed + jnp.dot(
            weight.astype(jnp.bfloat16), value_ref[...], preferred_element_type=jnp.float32
        )
    return total, summed


def first_kernel(query_segment_ref, key_segment_ref, query_ref, *refs, blocks, scale):
    key_refs = refs[:blocks]
    value_refs = refs[blocks : 2 * blocks]
    peak_ref, total_ref, summed_ref = refs[2 * blocks :]
    query = query_ref[...]
    query_segment = query_segment_ref[...]

    def scores(slot):
        return masked_scores(
            query, query_segment, key_segment_ref, key_refs[slot], slot, slot == 0, scale
        )

    peak = jnp.max(scores(0), axis=1, keepdims=True)
    for slot in range(1, blocks):
        peak = jnp.maximum(peak, jnp.max(scores(slot), axis=1, keepdims=True))
    total = jnp.zeros(peak.shape, jnp.float32)
    summed = jnp.zeros(summed_ref.shape, jnp.float32)
    total, summed = accumulate(scores, value_refs, peak, total, summed)
    peak_ref[...] = jnp.broadcast_to(peak, peak_ref.shape)
    total_ref[...] = jnp.broadcast_to(total, total_ref.shape)
    summed_ref[...] = summed


def second_kernel(
    query_segment_ref, key_segment_ref, query_ref, peak_ref, total_ref, summed_ref, *refs,
    blocks, scale,
):
    key_refs = refs[:blocks]
    value_refs = refs[blocks : 2 * blocks]
    out_ref = refs[2 * blocks]
    query = query_ref[...]
    query_segment = query_segment_ref[...]

    def scores(slot):
        return masked_scores(
            query, query_segment, key_segment_ref, key_refs[slot], slot, False, scale
        )

    first_peak = peak_ref[:, :1]
    peak = first_peak
    for slot in range(blocks):
        peak = jnp.maximum(peak, jnp.max(scores(slot), axis=1, keepdims=True))
    factor = jnp.exp(first_peak - peak)
    total = total_ref[:, :1] * factor
    summed = summed_ref[...] * factor
    total, summed = accumulate(scores, value_refs, peak, total, summed)
    out_ref[...] = (summed / total).astype(out_ref.dtype)


def attend(query, query_segment, key_segment, first, second, local_heads):
    rows = query.shape[0]
    grid = (local_heads, TOPK)
    combos = local_heads * TOPK
    scale = 1.0 / math.sqrt(HD)
    tile = pl.BlockSpec((rows, HD), lambda h, e: (0, e * local_heads + h))

    def column_spec(base):
        return pl.BlockSpec((rows, HD), lambda h, e: (0, base + h))

    def common(sources):
        specs = [
            pl.BlockSpec((rows, 1), lambda h, e: (0, 0)),
            pl.BlockSpec((len(sources), rows), lambda h, e: (0, 0)),
            tile,
        ]
        return specs

    def block_specs(sources):
        keys = [column_spec(base) for _, base in sources]
        values = [column_spec(base + local_heads) for _, base in sources]
        arrays = [array for array, _ in sources]
        return keys + values, arrays + arrays

    def cost(blocks):
        return pl.CostEstimate(
            flops=combos * 3 * blocks * 2 * rows * rows * HD,
            transcendentals=combos * blocks * rows * rows,
            bytes_accessed=query.size * 2 + blocks * rows * 2 * local_heads * HD * 2
            + 3 * combos * rows * HD * 4,
        )

    stats = jax.ShapeDtypeStruct((rows, combos * HD), jnp.float32)
    specs, arrays = block_specs(first)
    peak, total, summed = pl.pallas_call(
        functools.partial(first_kernel, blocks=len(first), scale=scale),
        grid=grid,
        in_specs=common(first) + specs,
        out_specs=(tile, tile, tile),
        out_shape=(stats, stats, stats),
        cost_estimate=cost(len(first)),
        name="first_blocks",
    )(query_segment, key_segment[0], query, *arrays)
    specs, arrays = block_specs(second)
    return pl.pallas_call(
        functools.partial(second_kernel, blocks=len(second), scale=scale),
        grid=grid,
        in_specs=common(second) + [tile, tile, tile] + specs,
        out_specs=tile,
        out_shape=jax.ShapeDtypeStruct(query.shape, jnp.bfloat16),
        cost_estimate=cost(len(second)),
        name="second_blocks",
    )(query_segment, key_segment[1], query, peak, total, summed, *arrays)


def body(tokens, key_weight, value_weight, queries, prompt_pages, page_table):
    block_rows = tokens.shape[0]
    width = key_weight.shape[1]
    local_heads = width // HD
    devices = lax.axis_size("seq")
    first_row = lax.axis_index("seq") * block_rows
    positions = first_row + jnp.arange(block_rows, dtype=jnp.int32)
    segment, offsets = segment_info(positions, prompt_pages)
    piece = lax.all_gather(tokens, "tp", axis=0, tiled=True)
    key_value = project(piece, key_weight, value_weight, offsets)
    direct = (1, 3, 5, 6)
    sent = {distance: from_behind(key_value, "seq", distance) for distance in direct}
    relayed = [distance for distance in range(2, BACK + 1) if distance not in direct]
    onward = from_behind(
        jnp.concatenate([sent[distance - 1] for distance in relayed], axis=1), "seq", 1
    )
    span = 2 * local_heads
    first = [(key_value, 0)] + [(sent[distance], 0) for distance in direct]
    second = [(onward, span * index) for index in range(len(relayed))]
    order = [0] + list(direct) + relayed
    key_place = positions[None, :] - block_rows * jnp.asarray(order, jnp.int32)[:, None]
    key_segment, _ = segment_info(key_place.reshape(-1), prompt_pages)
    key_segment = jnp.where(key_place >= 0, key_segment.reshape(len(order), block_rows), -1)
    key_segment = (key_segment[: len(first)], key_segment[len(first) :])
    query = queries.reshape(block_rows, TOPK * width)
    query_segment = segment[:, None]
    attended = attend(query, query_segment, key_segment, first, second, local_heads)
    attended = attended.reshape(block_rows, TOPK, width)
    pages_dev = block_rows // PAGE
    capacity = max(1, pages_dev // devices)
    owner = page_table // pages_dev
    place_on_owner = page_table % pages_dev
    page_order = jnp.arange(pages_dev, dtype=jnp.int32)
    earlier = (owner[:, None] == owner[None, :]) & (page_order[None, :] < page_order[:, None])
    rank = jnp.sum(earlier.astype(jnp.int32), axis=1)
    target = (owner[None, None, :] == jnp.arange(devices, dtype=jnp.int32)[:, None, None]) & (
        rank[None, None, :] == jnp.arange(capacity, dtype=jnp.int32)[None, :, None]
    )
    pages = key_value.reshape(pages_dev, PAGE, 2, width)
    page_index = jnp.sum(jnp.where(target, page_order[None, None, :], 0), axis=2)
    outgoing = pages[page_index.reshape(-1)]
    labels = jnp.sum(jnp.where(target, place_on_owner[None, None, :] + 1, 0), axis=2) - 1
    incoming = lax.all_to_all(outgoing, "seq", split_axis=0, concat_axis=0, tiled=True)
    arrived = lax.all_to_all(labels, "seq", split_axis=0, concat_axis=0, tiled=True)
    slots = jnp.arange(devices * capacity, dtype=jnp.int32)
    arrived = arrived.reshape(devices * capacity, 1)
    source_slot = jnp.sum(
        jnp.where(arrived == page_order[None, :], slots[:, None], 0), axis=0
    )
    cache = incoming[source_slot]
    return (attended, cache)


def solution(mesh):
    in_specs = (P("seq", "tp"), P(None, "tp"), P(None, "tp"), P("seq", None, "tp"), P(), P("seq"))
    out_specs = (P("seq", None, "tp"), P("seq", None, None, "tp"))
    return jax.shard_map(body, mesh=mesh, in_specs=in_specs, out_specs=out_specs, check_vma=False)
```

```python
import functools
import math

import jax
import jax.numpy as jnp
from jax import lax
from jax.experimental import pallas as pl
from jax.experimental.pallas import tpu as pltpu
from jax.sharding import PartitionSpec as P


HD = 128
TOPK = 2
PAGE = 16
BACK = 6


def from_behind(value, axis, by):
    peers = lax.axis_size(axis)
    pairs = [(i, i + by) for i in range(peers) if 0 <= i + by < peers]
    return lax.ppermute(value, axis, pairs)


def segment_info(positions, prompt_pages):
    ends = PAGE * jnp.cumsum(prompt_pages)
    below = ends[None, :] <= positions[:, None]
    segment = jnp.sum(below.astype(jnp.int32), axis=1)
    start = jnp.max(jnp.where(below, ends[None, :], 0), axis=1)
    return (segment, positions - start)


def project_kernel(piece_ref, key_weight_ref, value_weight_ref, cosine_ref, sine_ref, out_ref):
    rows = out_ref.shape[0]
    width = key_weight_ref.shape[1]
    share = piece_ref.shape[1]
    keys = jnp.zeros((rows, width), jnp.float32)
    values = jnp.zeros((rows, width), jnp.float32)
    for part in range(piece_ref.shape[0] // rows):
        chunk = piece_ref[part * rows : (part + 1) * rows, :]
        keys = keys + jnp.dot(
            chunk, key_weight_ref[part * share : (part + 1) * share, :],
            preferred_element_type=jnp.float32,
        )
        values = values + jnp.dot(
            chunk, value_weight_ref[part * share : (part + 1) * share, :],
            preferred_element_type=jnp.float32,
        )
    cosine = cosine_ref[...]
    sine = sine_ref[...]
    for head in range(width // HD):
        raw = keys[:, head * HD : (head + 1) * HD]
        turned = raw * cosine + pltpu.roll(raw, HD // 2, 1) * sine
        out_ref[:, head * HD : (head + 1) * HD] = turned.astype(out_ref.dtype)
    out_ref[:, width:] = values.astype(out_ref.dtype)


def project(piece, key_weight, value_weight, offsets):
    rows = offsets.shape[0]
    width = key_weight.shape[1]
    half = HD // 2
    inverse = 10000.0 ** (-(2.0 * jnp.arange(half, dtype=jnp.float32)) / HD)
    angle = offsets.astype(jnp.float32)[:, None] * inverse[None, :]
    cosine = jnp.cos(angle)
    sine = jnp.sin(angle)
    cosine = jnp.concatenate([cosine, cosine], axis=1)
    sine = jnp.concatenate([-sine, sine], axis=1)
    cost = pl.CostEstimate(
        flops=2 * 2 * rows * key_weight.shape[0] * width,
        transcendentals=0,
        bytes_accessed=piece.size * 2 + 2 * key_weight.size * 2 + rows * 2 * width * 2,
    )
    return pl.pallas_call(
        project_kernel,
        out_shape=jax.ShapeDtypeStruct((rows, 2 * width), jnp.bfloat16),
        cost_estimate=cost,
        name="project_rotate",
    )(piece, key_weight, value_weight, cosine, sine)


def masked_scores(query, query_segment, key_segment_ref, key_ref, slot, diagonal, scale):
    rows = query.shape[0]
    product = lax.dot_general(
        query, key_ref[...], (((1,), (1,)), ((), ())), preferred_element_type=jnp.float32
    )
    allowed = query_segment == key_segment_ref[pl.ds(slot, 1), :]
    if diagonal:
        row = lax.broadcasted_iota(jnp.int32, (rows, rows), 0)
        col = lax.broadcasted_iota(jnp.int32, (rows, rows), 1)
        allowed = allowed & (col <= row)
    return jnp.where(allowed, product * scale, -jnp.inf)


def accumulate(scores, value_refs, peak, total, summed):
    for slot, value_ref in enumerate(value_refs):
        weight = jnp.exp(scores(slot) - peak)
        total = total + jnp.sum(weight, axis=1, keepdims=True)
        summed = summed + jnp.dot(
            weight.astype(jnp.bfloat16), value_ref[...], preferred_element_type=jnp.float32
        )
    return total, summed


def first_kernel(query_segment_ref, key_segment_ref, query_ref, *refs, blocks, scale):
    key_refs = refs[:blocks]
    value_refs = refs[blocks : 2 * blocks]
    stats_ref, summed_ref = refs[2 * blocks :]
    query = query_ref[...]
    query_segment = query_segment_ref[...]

    def scores(slot):
        return masked_scores(
            query, query_segment, key_segment_ref, key_refs[slot], slot, slot == 0, scale
        )

    peak = jnp.max(scores(0), axis=1, keepdims=True)
    for slot in range(1, blocks):
        peak = jnp.maximum(peak, jnp.max(scores(slot), axis=1, keepdims=True))
    total = jnp.zeros(peak.shape, jnp.float32)
    summed = jnp.zeros(summed_ref.shape, jnp.float32)
    total, summed = accumulate(scores, value_refs, peak, total, summed)
    combos = stats_ref.shape[1] // 2
    combo = pl.program_id(1) * pl.num_programs(0) + pl.program_id(0)
    lane = lax.broadcasted_iota(jnp.int32, stats_ref.shape, 1)

    @pl.when(combo == 0)
    def _():
        stats_ref[...] = jnp.zeros(stats_ref.shape, jnp.float32)

    stats = jnp.where(lane == combo, peak, stats_ref[...])
    stats_ref[...] = jnp.where(lane == combo + combos, total, stats)
    summed_ref[...] = summed


def second_kernel(
    query_segment_ref, key_segment_ref, query_ref, stats_ref, summed_ref, source_ref, out_ref,
    *, blocks, scale, local_heads,
):
    query_segment = query_segment_ref[...]
    stats = stats_ref[...]
    lane = lax.broadcasted_iota(jnp.int32, stats.shape, 1)
    combos = stats.shape[1] // 2
    span = 2 * local_heads * HD
    for expert in range(TOPK):
        for head in range(local_heads):
            combo = expert * local_heads + head
            columns = slice(combo * HD, (combo + 1) * HD)
            query = query_ref[:, columns]

            def scores(slot):
                key = source_ref[:, slot * span + head * HD : slot * span + (head + 1) * HD]
                product = lax.dot_general(
                    query, key, (((1,), (1,)), ((), ())), preferred_element_type=jnp.float32
                )
                allowed = query_segment == key_segment_ref[pl.ds(slot, 1), :]
                return jnp.where(allowed, product * scale, -jnp.inf)

            first_peak = jnp.sum(jnp.where(lane == combo, stats, 0.0), axis=1, keepdims=True)
            first_total = jnp.sum(
                jnp.where(lane == combo + combos, stats, 0.0), axis=1, keepdims=True
            )
            peak = first_peak
            for slot in range(blocks):
                peak = jnp.maximum(peak, jnp.max(scores(slot), axis=1, keepdims=True))
            factor = jnp.exp(first_peak - peak)
            total = first_total * factor
            summed = summed_ref[:, columns] * factor
            for slot in range(blocks):
                weight = jnp.exp(scores(slot) - peak)
                total = total + jnp.sum(weight, axis=1, keepdims=True)
                start = slot * span + (local_heads + head) * HD
                summed = summed + jnp.dot(
                    weight.astype(jnp.bfloat16),
                    source_ref[:, start : start + HD],
                    preferred_element_type=jnp.float32,
                )
            out_ref[:, columns] = (summed / total).astype(out_ref.dtype)


def attend(query, query_segment, key_segment, first, second, local_heads):
    rows = query.shape[0]
    grid = (local_heads, TOPK)
    combos = local_heads * TOPK
    scale = 1.0 / math.sqrt(HD)
    tile = pl.BlockSpec((rows, HD), lambda h, e: (0, e * local_heads + h))

    def column_spec(base):
        return pl.BlockSpec((rows, HD), lambda h, e: (0, base + h))

    def common(sources):
        specs = [
            pl.BlockSpec((rows, 1), lambda h, e: (0, 0)),
            pl.BlockSpec((len(sources), rows), lambda h, e: (0, 0)),
            tile,
        ]
        return specs

    def block_specs(sources):
        keys = [column_spec(base) for _, base in sources]
        values = [column_spec(base + local_heads) for _, base in sources]
        arrays = [array for array, _ in sources]
        return keys + values, arrays + arrays

    def cost(blocks):
        return pl.CostEstimate(
            flops=combos * 3 * blocks * 2 * rows * rows * HD,
            transcendentals=combos * blocks * rows * rows,
            bytes_accessed=query.size * 2 + blocks * rows * 2 * local_heads * HD * 2
            + 3 * combos * rows * HD * 4,
        )

    stats_shape = jax.ShapeDtypeStruct((rows, 2 * combos), jnp.float32)
    summed_shape = jax.ShapeDtypeStruct((rows, combos * HD), jnp.float32)
    stats_spec = pl.BlockSpec((rows, 2 * combos), lambda h, e: (0, 0))
    specs, arrays = block_specs(first)
    stats, summed = pl.pallas_call(
        functools.partial(first_kernel, blocks=len(first), scale=scale),
        grid=grid,
        in_specs=common(first) + specs,
        out_specs=(stats_spec, tile),
        out_shape=(stats_shape, summed_shape),
        cost_estimate=cost(len(first)),
        name="first_blocks",
    )(query_segment, key_segment[0], query, *arrays)
    source = second[0][0]
    assert all(array is source for array, _ in second)
    return pl.pallas_call(
        functools.partial(
            second_kernel, blocks=len(second), scale=scale, local_heads=local_heads
        ),
        out_shape=jax.ShapeDtypeStruct(query.shape, jnp.bfloat16),
        cost_estimate=cost(len(second)),
        name="second_blocks",
    )(query_segment, key_segment[1], query, stats, summed, source)


def body(tokens, key_weight, value_weight, queries, prompt_pages, page_table):
    block_rows = tokens.shape[0]
    width = key_weight.shape[1]
    local_heads = width // HD
    devices = lax.axis_size("seq")
    first_row = lax.axis_index("seq") * block_rows
    positions = first_row + jnp.arange(block_rows, dtype=jnp.int32)
    segment, offsets = segment_info(positions, prompt_pages)
    piece = lax.all_gather(tokens, "tp", axis=0, tiled=True)
    key_value = project(piece, key_weight, value_weight, offsets)
    direct = (1, 3, 5, 6)
    sent = {distance: from_behind(key_value, "seq", distance) for distance in direct}
    relayed = [distance for distance in range(2, BACK + 1) if distance not in direct]
    onward = from_behind(
        jnp.concatenate([sent[distance - 1] for distance in relayed], axis=1), "seq", 1
    )
    span = 2 * local_heads
    first = [(key_value, 0)] + [(sent[distance], 0) for distance in direct]
    second = [(onward, span * index) for index in range(len(relayed))]
    order = [0] + list(direct) + relayed
    key_place = positions[None, :] - block_rows * jnp.asarray(order, jnp.int32)[:, None]
    key_segment, _ = segment_info(key_place.reshape(-1), prompt_pages)
    key_segment = jnp.where(key_place >= 0, key_segment.reshape(len(order), block_rows), -1)
    key_segment = (key_segment[: len(first)], key_segment[len(first) :])
    query = queries.reshape(block_rows, TOPK * width)
    query_segment = segment[:, None]
    attended = attend(query, query_segment, key_segment, first, second, local_heads)
    attended = attended.reshape(block_rows, TOPK, width)
    pages_dev = block_rows // PAGE
    capacity = max(1, pages_dev // devices)
    owner = page_table // pages_dev
    place_on_owner = page_table % pages_dev
    page_order = jnp.arange(pages_dev, dtype=jnp.int32)
    earlier = (owner[:, None] == owner[None, :]) & (page_order[None, :] < page_order[:, None])
    rank = jnp.sum(earlier.astype(jnp.int32), axis=1)
    target = (owner[None, None, :] == jnp.arange(devices, dtype=jnp.int32)[:, None, None]) & (
        rank[None, None, :] == jnp.arange(capacity, dtype=jnp.int32)[None, :, None]
    )
    pages = key_value.reshape(pages_dev, PAGE, 2 * width)
    page_index = jnp.sum(jnp.where(target, page_order[None, None, :], 0), axis=2)
    outgoing = pages[page_index.reshape(-1)]
    labels = jnp.sum(jnp.where(target, place_on_owner[None, None, :] + 1, 0), axis=2) - 1
    incoming = lax.all_to_all(outgoing, "seq", split_axis=0, concat_axis=0, tiled=True)
    arrived = lax.all_to_all(labels, "seq", split_axis=0, concat_axis=0, tiled=True)
    slots = jnp.arange(devices * capacity, dtype=jnp.int32)
    arrived = arrived.reshape(devices * capacity, 1)
    source_slot = jnp.sum(
        jnp.where(arrived == page_order[None, :], slots[:, None], 0), axis=0
    )
    cache = incoming[source_slot].reshape(pages_dev, PAGE, 2, width)
    return (attended, cache)


def solution(mesh):
    in_specs = (P("seq", "tp"), P(None, "tp"), P(None, "tp"), P("seq", None, "tp"), P(), P("seq"))
    out_specs = (P("seq", None, "tp"), P("seq", None, None, "tp"))
    return jax.shard_map(body, mesh=mesh, in_specs=in_specs, out_specs=out_specs, check_vma=False)
```

```python
import functools
import math

import jax
import jax.numpy as jnp
from jax import lax
from jax.experimental import pallas as pl
from jax.experimental.pallas import tpu as pltpu
from jax.sharding import PartitionSpec as P


HD = 128
TOPK = 2
PAGE = 16
BACK = 6


def from_behind(value, axis, by):
    peers = lax.axis_size(axis)
    pairs = [(i, i + by) for i in range(peers) if 0 <= i + by < peers]
    return lax.ppermute(value, axis, pairs)


def segment_info(positions, prompt_pages):
    ends = PAGE * jnp.cumsum(prompt_pages)
    below = ends[None, :] <= positions[:, None]
    segment = jnp.sum(below.astype(jnp.int32), axis=1)
    start = jnp.max(jnp.where(below, ends[None, :], 0), axis=1)
    return (segment, positions - start)


def project_kernel(piece_ref, key_weight_ref, value_weight_ref, cosine_ref, sine_ref, out_ref):
    rows = out_ref.shape[0]
    width = key_weight_ref.shape[1]
    share = piece_ref.shape[1]
    keys = jnp.zeros((rows, width), jnp.float32)
    values = jnp.zeros((rows, width), jnp.float32)
    for part in range(piece_ref.shape[0] // rows):
        chunk = piece_ref[part * rows : (part + 1) * rows, :]
        keys = keys + jnp.dot(
            chunk, key_weight_ref[part * share : (part + 1) * share, :],
            preferred_element_type=jnp.float32,
        )
        values = values + jnp.dot(
            chunk, value_weight_ref[part * share : (part + 1) * share, :],
            preferred_element_type=jnp.float32,
        )
    cosine = cosine_ref[...]
    sine = sine_ref[...]
    for head in range(width // HD):
        raw = keys[:, head * HD : (head + 1) * HD]
        turned = raw * cosine + pltpu.roll(raw, HD // 2, 1) * sine
        out_ref[:, head * HD : (head + 1) * HD] = turned.astype(out_ref.dtype)
    out_ref[:, width:] = values.astype(out_ref.dtype)


def project(piece, key_weight, value_weight, offsets):
    rows = offsets.shape[0]
    width = key_weight.shape[1]
    half = HD // 2
    inverse = 10000.0 ** (-(2.0 * jnp.arange(half, dtype=jnp.float32)) / HD)
    angle = offsets.astype(jnp.float32)[:, None] * inverse[None, :]
    cosine = jnp.cos(angle)
    sine = jnp.sin(angle)
    cosine = jnp.concatenate([cosine, cosine], axis=1)
    sine = jnp.concatenate([-sine, sine], axis=1)
    cost = pl.CostEstimate(
        flops=2 * 2 * rows * key_weight.shape[0] * width,
        transcendentals=0,
        bytes_accessed=piece.size * 2 + 2 * key_weight.size * 2 + rows * 2 * width * 2,
    )
    return pl.pallas_call(
        project_kernel,
        out_shape=jax.ShapeDtypeStruct((rows, 2 * width), jnp.bfloat16),
        cost_estimate=cost,
        name="project_rotate",
    )(piece, key_weight, value_weight, cosine, sine)


def masked_scores(query, query_segment, key_segment_ref, key_ref, slot, diagonal, scale):
    rows = query.shape[0]
    product = lax.dot_general(
        query, key_ref[...], (((1,), (1,)), ((), ())), preferred_element_type=jnp.float32
    )
    allowed = query_segment == key_segment_ref[pl.ds(slot, 1), :]
    if diagonal:
        row = lax.broadcasted_iota(jnp.int32, (rows, rows), 0)
        col = lax.broadcasted_iota(jnp.int32, (rows, rows), 1)
        allowed = allowed & (col <= row)
    return jnp.where(allowed, product * scale, -jnp.inf)


def accumulate(scores, value_refs, peak, total, summed):
    for slot, value_ref in enumerate(value_refs):
        weight = jnp.exp(scores(slot) - peak)
        total = total + jnp.sum(weight, axis=1, keepdims=True)
        summed = summed + jnp.dot(
            weight.astype(jnp.bfloat16), value_ref[...], preferred_element_type=jnp.float32
        )
    return total, summed


def first_kernel(query_segment_ref, key_segment_ref, query_ref, *refs, blocks, scale):
    key_refs = refs[:blocks]
    value_refs = refs[blocks : 2 * blocks]
    stats_ref, summed_ref = refs[2 * blocks :]
    query = query_ref[...]
    query_segment = query_segment_ref[...]

    def scores(slot):
        return masked_scores(
            query, query_segment, key_segment_ref, key_refs[slot], slot, slot == 0, scale
        )

    peak = jnp.max(scores(0), axis=1, keepdims=True)
    for slot in range(1, blocks):
        peak = jnp.maximum(peak, jnp.max(scores(slot), axis=1, keepdims=True))
    total = jnp.zeros(peak.shape, jnp.float32)
    summed = jnp.zeros(summed_ref.shape, jnp.float32)
    total, summed = accumulate(scores, value_refs, peak, total, summed)
    combos = stats_ref.shape[1] // 2
    combo = pl.program_id(1) * pl.num_programs(0) + pl.program_id(0)
    lane = lax.broadcasted_iota(jnp.int32, stats_ref.shape, 1)

    @pl.when(combo == 0)
    def _():
        stats_ref[...] = jnp.zeros(stats_ref.shape, jnp.float32)

    stats = jnp.where(lane == combo, peak, stats_ref[...])
    stats_ref[...] = jnp.where(lane == combo + combos, total, stats)
    summed_ref[...] = summed


def second_kernel(
    query_segment_ref, key_segment_ref, query_ref, stats_ref, summed_ref, source_ref, out_ref,
    *, blocks, scale, local_heads,
):
    query_segment = query_segment_ref[...]
    stats = stats_ref[...]
    lane = lax.broadcasted_iota(jnp.int32, stats.shape, 1)
    combos = stats.shape[1] // 2
    span = 2 * local_heads * HD
    for expert in range(TOPK):
        for head in range(local_heads):
            combo = expert * local_heads + head
            columns = slice(combo * HD, (combo + 1) * HD)
            query = query_ref[:, columns]

            def scores(slot):
                key = source_ref[:, slot * span + head * HD : slot * span + (head + 1) * HD]
                product = lax.dot_general(
                    query, key, (((1,), (1,)), ((), ())), preferred_element_type=jnp.float32
                )
                allowed = query_segment == key_segment_ref[pl.ds(slot, 1), :]
                return jnp.where(allowed, product * scale, -jnp.inf)

            first_peak = jnp.sum(jnp.where(lane == combo, stats, 0.0), axis=1, keepdims=True)
            first_total = jnp.sum(
                jnp.where(lane == combo + combos, stats, 0.0), axis=1, keepdims=True
            )
            peak = first_peak
            for slot in range(blocks):
                peak = jnp.maximum(peak, jnp.max(scores(slot), axis=1, keepdims=True))
            factor = jnp.exp(first_peak - peak)
            total = first_total * factor
            summed = summed_ref[:, columns] * factor
            for slot in range(blocks):
                weight = jnp.exp(scores(slot) - peak)
                total = total + jnp.sum(weight, axis=1, keepdims=True)
                start = slot * span + (local_heads + head) * HD
                summed = summed + jnp.dot(
                    weight.astype(jnp.bfloat16),
                    source_ref[:, start : start + HD],
                    preferred_element_type=jnp.float32,
                )
            out_ref[:, expert, head * HD : (head + 1) * HD] = (summed / total).astype(out_ref.dtype)


def attend(query, query_segment, key_segment, first, second, local_heads):
    rows = query.shape[0]
    grid = (local_heads, TOPK)
    combos = local_heads * TOPK
    scale = 1.0 / math.sqrt(HD)
    tile = pl.BlockSpec((rows, HD), lambda h, e: (0, e * local_heads + h))

    def column_spec(base):
        return pl.BlockSpec((rows, HD), lambda h, e: (0, base + h))

    def common(sources):
        specs = [
            pl.BlockSpec((rows, 1), lambda h, e: (0, 0)),
            pl.BlockSpec((len(sources), rows), lambda h, e: (0, 0)),
            tile,
        ]
        return specs

    def block_specs(sources):
        keys = [column_spec(base) for _, base in sources]
        values = [column_spec(base + local_heads) for _, base in sources]
        arrays = [array for array, _ in sources]
        return keys + values, arrays + arrays

    def cost(blocks):
        return pl.CostEstimate(
            flops=combos * 3 * blocks * 2 * rows * rows * HD,
            transcendentals=combos * blocks * rows * rows,
            bytes_accessed=query.size * 2 + blocks * rows * 2 * local_heads * HD * 2
            + 3 * combos * rows * HD * 4,
        )

    stats_shape = jax.ShapeDtypeStruct((rows, 2 * combos), jnp.float32)
    summed_shape = jax.ShapeDtypeStruct((rows, combos * HD), jnp.float32)
    stats_spec = pl.BlockSpec((rows, 2 * combos), lambda h, e: (0, 0))
    specs, arrays = block_specs(first)
    stats, summed = pl.pallas_call(
        functools.partial(first_kernel, blocks=len(first), scale=scale),
        grid=grid,
        in_specs=common(first) + specs,
        out_specs=(stats_spec, tile),
        out_shape=(stats_shape, summed_shape),
        cost_estimate=cost(len(first)),
        name="first_blocks",
    )(query_segment, key_segment[0], query, *arrays)
    source = second[0][0]
    assert all(array is source for array, _ in second)
    return pl.pallas_call(
        functools.partial(
            second_kernel, blocks=len(second), scale=scale, local_heads=local_heads
        ),
        out_shape=jax.ShapeDtypeStruct((rows, TOPK, combos * HD // TOPK), jnp.bfloat16),
        cost_estimate=cost(len(second)),
        name="second_blocks",
    )(query_segment, key_segment[1], query, stats, summed, source)


def body(tokens, key_weight, value_weight, queries, prompt_pages, page_table):
    block_rows = tokens.shape[0]
    width = key_weight.shape[1]
    local_heads = width // HD
    devices = lax.axis_size("seq")
    first_row = lax.axis_index("seq") * block_rows
    positions = first_row + jnp.arange(block_rows, dtype=jnp.int32)
    segment, offsets = segment_info(positions, prompt_pages)
    piece = lax.all_gather(tokens, "tp", axis=0, tiled=True)
    key_value = project(piece, key_weight, value_weight, offsets)
    direct = (1, 3, 5, 6)
    sent = {distance: from_behind(key_value, "seq", distance) for distance in direct}
    relayed = [distance for distance in range(2, BACK + 1) if distance not in direct]
    onward = from_behind(
        jnp.concatenate([sent[distance - 1] for distance in relayed], axis=1), "seq", 1
    )
    span = 2 * local_heads
    first = [(key_value, 0)] + [(sent[distance], 0) for distance in direct]
    second = [(onward, span * index) for index in range(len(relayed))]
    order = [0] + list(direct) + relayed
    key_place = positions[None, :] - block_rows * jnp.asarray(order, jnp.int32)[:, None]
    key_segment, _ = segment_info(key_place.reshape(-1), prompt_pages)
    key_segment = jnp.where(key_place >= 0, key_segment.reshape(len(order), block_rows), -1)
    key_segment = (key_segment[: len(first)], key_segment[len(first) :])
    query = queries.reshape(block_rows, TOPK * width)
    query_segment = segment[:, None]
    attended = attend(query, query_segment, key_segment, first, second, local_heads)
    pages_dev = block_rows // PAGE
    capacity = max(1, pages_dev // devices)
    owner = page_table // pages_dev
    place_on_owner = page_table % pages_dev
    page_order = jnp.arange(pages_dev, dtype=jnp.int32)
    earlier = (owner[:, None] == owner[None, :]) & (page_order[None, :] < page_order[:, None])
    rank = jnp.sum(earlier.astype(jnp.int32), axis=1)
    target = (owner[None, None, :] == jnp.arange(devices, dtype=jnp.int32)[:, None, None]) & (
        rank[None, None, :] == jnp.arange(capacity, dtype=jnp.int32)[None, :, None]
    )
    pages = key_value.reshape(pages_dev, PAGE, 2 * width)
    page_index = jnp.sum(jnp.where(target, page_order[None, None, :], 0), axis=2)
    outgoing = pages[page_index.reshape(-1)]
    labels = jnp.sum(jnp.where(target, place_on_owner[None, None, :] + 1, 0), axis=2) - 1
    incoming = lax.all_to_all(outgoing, "seq", split_axis=0, concat_axis=0, tiled=True)
    arrived = lax.all_to_all(labels, "seq", split_axis=0, concat_axis=0, tiled=True)
    slots = jnp.arange(devices * capacity, dtype=jnp.int32)
    arrived = arrived.reshape(devices * capacity, 1)
    source_slot = jnp.sum(
        jnp.where(arrived == page_order[None, :], slots[:, None], 0), axis=0
    )
    cache = incoming[source_slot].reshape(pages_dev, PAGE, 2, width)
    return (attended, cache)


def solution(mesh):
    in_specs = (P("seq", "tp"), P(None, "tp"), P(None, "tp"), P("seq", None, "tp"), P(), P("seq"))
    out_specs = (P("seq", None, "tp"), P("seq", None, None, "tp"))
    return jax.shard_map(body, mesh=mesh, in_specs=in_specs, out_specs=out_specs, check_vma=False)
```
